128 devices in a mesh: lon: 16 (over y, x_hi, core), lat: 8 (over x_lo, z).
Axes of the slice: x: 4 (x_hi: 2, x_lo: 2; x = x_hi * 2 + x_lo), y: 4, z: 4, core: 2. Of those that a mesh axis runs over, the one named last changes fastest.
Arguments:
- anomalies: bfloat16 [16, 128, 80, 128], P('lat', 'lon'), may hold values from -6 to 6
- panel: float32 [16, 128, 128, 128], P('lat', 'lon'), may hold values from -6 to 6
- pair_code: int32 [16, 128, 9], P('lat', 'lon'), may hold values from 0 to 8, as said below
- pair_offset: int32 [2, 16, 128, 9], P(None, 'lat', 'lon'), may hold values from -16 to 16, as said below
Outputs:
- first_product: float32 [16, 128, 128, 128], P('lat', 'lon')
- second_product: float32 [16, 128, 128, 128], P('lat', 'lon')
The draws below stay inside these ranges and needn't reach their ends.
Inputs may be any that keep to these rules, and one draw needn't show every extreme that they name: `pair_code`: slot 0 of every block holds code 4, the block itself; its other slots hold the eight neighbouring blocks' codes, each once. `pair_offset`: for code g the offsets are exactly (g // 3 - 1) * 8 and (g % 3 - 1) * 16.
All inputs are finite; a program needn't handle non-finite values.
Results may differ from the reference program's by a relative error of at most 0.0003.
Values may be sent and summed in bfloat16 or wider, within the bound.
No kernel may reach another device: no remote copies, remote signals or barrier semaphores. Data moves between devices by JAX's collectives and lax.ppermute only.
A program may use at most 128 MiB of HBM per device.

```python
import jax
import jax.numpy as jnp
from jax import lax

K = 80
COLS = 128
STRIDE = 16
R = 128
PAIRS = 9
RADIUS = 4
NBLAT = 16
NBLON = 128


def neighbour_codes(key):
    others = jnp.array([0, 1, 2, 3, 5, 6, 7, 8], dtype=jnp.int32)
    scores = jax.random.randint(jax.random.fold_in(key, 11), (NBLAT, NBLON, 8), 0, 1 << 20) * 8 + jnp.arange(8, dtype=jnp.int32)
    ranking = jnp.argsort(scores, axis=-1, stable=True)
    picked = others[ranking[..., :PAIRS - 1]]
    itself = jnp.full((NBLAT, NBLON, 1), 4, jnp.int32)
    return jnp.concatenate([itself, picked], axis=-1)


def draw_pair_code(key, part):
    return neighbour_codes(key)


def draw_pair_offset(key, part):
    codes_all = neighbour_codes(key)
    north = codes_all // 3 - 1
    eastward = codes_all % 3 - 1
    return jnp.stack([COLS // STRIDE * north, STRIDE * eastward]).astype(jnp.int32)


def shard_levels(rng, shape, pieces, smallest, high):
    level = 1.0
    for axis_at, blocks in pieces:
        heights = jax.random.uniform(jax.random.fold_in(jax.random.fold_in(rng, 6), axis_at), (blocks,), jnp.float32, smallest / len(pieces), high / len(pieces))
        level = level * jnp.repeat(jnp.exp(heights), shape[axis_at] // blocks).reshape((-1,) + (1,) * (len(shape) - 1 - axis_at))
    return level


def centred(stream_key, extent, deviation, most, pieces=(), kind=jnp.bfloat16):
    loudness = shard_levels(stream_key, extent, pieces, -0.22, 0.18) if pieces else 1.0
    drawn = jax.random.normal(stream_key, extent, jnp.float32) * deviation * loudness
    return jnp.minimum(jnp.maximum(drawn, -most), most).astype(kind)


def setup_inputs(seed: int = 0) -> dict:
    keys = jax.random.split(jax.random.key(seed), 5)
    anomalies = centred(keys[0], (NBLAT, NBLON, K, COLS), 1.0, 6.0, ((0, 8), (1, 16)))
    panel = centred(keys[1], (NBLAT, NBLON, COLS, R), 1.0, 6.0, ((0, 8), (1, 16)), jnp.float32)
    pair_code = draw_pair_code(jax.random.fold_in(keys[4], 71), 0)
    pair_offset = draw_pair_offset(jax.random.fold_in(keys[4], 71), 0)
    return dict(anomalies=anomalies, panel=panel, pair_code=pair_code, pair_offset=pair_offset)


def gaspari_cohn(shift_rows, shift_cols):
    position = jnp.arange(COLS)
    row_within = position // STRIDE
    col_within = position % STRIDE
    delta_rows = shift_rows[..., None, None] + (row_within[None, :] - row_within[:, None])
    delta_cols = shift_cols[..., None, None] + (col_within[None, :] - col_within[:, None])
    squared = (delta_rows * delta_rows + delta_cols * delta_cols).astype(jnp.float32)
    scaled = jnp.sqrt(squared + 0.25) / RADIUS
    inside = (((-0.25 * scaled + 0.5) * scaled + 0.625) * scaled - 5.0 / 3.0) * scaled * scaled + 1.0
    outside = ((((scaled / 12.0 - 0.5) * scaled + 0.625) * scaled + 5.0 / 3.0) * scaled - 5.0) * scaled + 4.0 - 2.0 / (3.0 * scaled)
    return jnp.where(scaled <= 1.0, inside, jnp.where(scaled <= 2.0, outside, 0.0))

def localized_product(anomalies, field_in, pair_code, pair_offset):
    member_pad = jnp.pad(anomalies.astype(jnp.float32), ((1, 1), (0, 0), (0, 0), (0, 0)))
    field_pad = jnp.pad(field_in, ((1, 1), (0, 0), (0, 0), (0, 0)))
    lon_index = jnp.arange(NBLON, dtype=jnp.int32)

    def one_row(lat_row):
        member_rows = lax.dynamic_slice_in_dim(member_pad, lat_row, 3, 0)
        field_rows = lax.dynamic_slice_in_dim(field_pad, lat_row, 3, 0)
        code_row = pair_code[lat_row]
        offset_rows = pair_offset[0][lat_row]
        offset_cols = pair_offset[1][lat_row]
        targets = member_rows[1]
        accumulated = jnp.zeros((NBLON, COLS, R), jnp.float32)
        for slot_index in range(PAIRS):
            codes_now = code_row[:, slot_index]
            row_pick = codes_now // 3
            col_pick = (lon_index + codes_now % 3 - 1) % NBLON
            source_members = member_rows[row_pick, col_pick]
            source_field = field_rows[row_pick, col_pick]
            gram_block = jnp.einsum('bki,bkj->bij', targets, source_members, precision=lax.Precision.HIGHEST)
            tile_block = gram_block * gaspari_cohn(offset_rows[:, slot_index], offset_cols[:, slot_index]) / (K - 1)
            accumulated = accumulated + jnp.einsum('bij,bjr->bir', tile_block, source_field, precision=lax.Precision.HIGHEST)
        return accumulated
    return lax.map(one_row, jnp.arange(NBLAT, dtype=jnp.int32))

def reference(anomalies, panel, pair_code, pair_offset):
    first_product = localized_product(anomalies, panel, pair_code, pair_offset)
    second_product = localized_product(anomalies, first_product, pair_code, pair_offset)
    return (first_product, second_product)
```

```python
import functools

import jax
import jax.numpy as jnp
from jax import lax
from jax.experimental import pallas as pl
from jax.experimental.pallas import tpu as pltpu
from jax.sharding import PartitionSpec as P

K = 80
COLS = 128
STRIDE = 16
RADIUS = 4
CODES = 9


def gaspari_cohn(shift_rows, shift_cols):
    position = jnp.arange(COLS)
    row_within = position // STRIDE
    col_within = position % STRIDE
    delta_rows = shift_rows[..., None, None] + (row_within[None, :] - row_within[:, None])
    delta_cols = shift_cols[..., None, None] + (col_within[None, :] - col_within[:, None])
    squared = (delta_rows * delta_rows + delta_cols * delta_cols).astype(jnp.float32)
    scaled = jnp.sqrt(squared + 0.25) / RADIUS
    inside = (
        ((-0.25 * scaled + 0.5) * scaled + 0.625) * scaled - 5.0 / 3.0
    ) * scaled * scaled + 1.0
    outside = (
        ((((scaled / 12.0 - 0.5) * scaled + 0.625) * scaled + 5.0 / 3.0) * scaled - 5.0) * scaled
        + 4.0
        - 2.0 / (3.0 * scaled)
    )
    return jnp.where(scaled <= 1.0, inside, jnp.where(scaled <= 2.0, outside, 0.0))


def taper_by_code():
    codes = jnp.arange(CODES, dtype=jnp.int32)
    shift_rows = (codes // 3 - 1) * (COLS // STRIDE)
    shift_cols = (codes % 3 - 1) * STRIDE
    return gaspari_cohn(shift_rows, shift_cols) / (K - 1)


def with_halo(cells):
    nlat = lax.axis_size("lat")
    nlon = lax.axis_size("lon")
    down = [(i, i + 1) for i in range(nlat - 1)]
    up = [(i + 1, i) for i in range(nlat - 1)]
    right = [(i, (i + 1) % nlon) for i in range(nlon)]
    left = [((i + 1) % nlon, i) for i in range(nlon)]

    def both(lat_pairs, lon_shift):
        return [
            (b * nlat + a, ((b + lon_shift) % nlon) * nlat + c)
            for a, c in lat_pairs
            for b in range(nlon)
        ]

    first_row, last_row = cells[:1], cells[-1:]
    north = lax.ppermute(last_row, "lat", down)
    south = lax.ppermute(first_row, "lat", up)
    west = lax.ppermute(cells[:, -1:], "lon", right)
    east = lax.ppermute(cells[:, :1], "lon", left)
    north_west = lax.ppermute(last_row[:, -1:], ("lon", "lat"), both(down, 1))
    north_east = lax.ppermute(last_row[:, :1], ("lon", "lat"), both(down, -1))
    south_west = lax.ppermute(first_row[:, -1:], ("lon", "lat"), both(up, 1))
    south_east = lax.ppermute(first_row[:, :1], ("lon", "lat"), both(up, -1))
    top = jnp.concatenate([north_west, north, north_east], axis=1)
    middle = jnp.concatenate([west, cells, east], axis=1)
    bottom = jnp.concatenate([south_west, south, south_east], axis=1)
    return jnp.concatenate([top, middle, bottom], axis=0)


def product_kernel(targets_ref, members_ref, high_ref, low_ref, taper_ref, out_ref):
    lat_blocks, lon_blocks = out_ref.shape[0], out_ref.shape[1]

    def one_block(t, carry):
        p = t // lon_blocks
        q = t % lon_blocks
        target = targets_ref[p, q]
        total = jnp.zeros(out_ref.shape[2:], jnp.float32)
        for code in range(CODES):
            dr, dc = code // 3, code % 3
            gram = jnp.dot(target, members_ref[p + dr, q + dc], preferred_element_type=jnp.float32)
            tile = gram * taper_ref[code]
            tile_high = tile.astype(jnp.bfloat16)
            tile_low = (tile - tile_high.astype(jnp.float32)).astype(jnp.bfloat16)
            field_high = high_ref[p + dr, q + dc]
            field_low = low_ref[p + dr, q + dc]
            total = total + jnp.dot(tile_high, field_high, preferred_element_type=jnp.float32)
            total = total + jnp.dot(tile_high, field_low, preferred_element_type=jnp.float32)
            total = total + jnp.dot(tile_low, field_high, preferred_element_type=jnp.float32)
        out_ref[p, q] = total
        return carry

    lax.fori_loop(0, lat_blocks * lon_blocks, one_block, 0)


def localized_product(targets, members_wide, field_in, taper):
    lat_blocks, lon_blocks, columns, rank = field_in.shape
    field_wide = with_halo(field_in)
    rounded = lax.reduce_precision(field_wide, exponent_bits=8, mantissa_bits=7)
    high = rounded.astype(jnp.bfloat16)
    low = (field_wide - rounded).astype(jnp.bfloat16)
    blocks = lat_blocks * lon_blocks
    flops = blocks * CODES * 2 * columns * (K * columns + 3 * columns * rank)
    moved = high.size * 4 + members_wide.size * 2 + targets.size * 2 + taper.size * 4 + field_in.size * 4
    vmem = pl.BlockSpec(memory_space=pltpu.VMEM)
    return pl.pallas_call(
        product_kernel,
        out_shape=jax.ShapeDtypeStruct(field_in.shape, jnp.float32),
        in_specs=[vmem] * 5,
        out_specs=vmem,
        cost_estimate=pl.CostEstimate(flops=flops, bytes_accessed=moved, transcendentals=0),
    )(targets, members_wide, high, low, taper)


def local(anomalies, panel, pair_code, pair_offset):
    del pair_code, pair_offset
    taper = taper_by_code()
    targets = jnp.swapaxes(anomalies, 2, 3)
    members_wide = with_halo(anomalies)
    first_product = localized_product(targets, members_wide, panel, taper)
    second_product = localized_product(targets, members_wide, first_product, taper)
    return (first_product, second_product)


def solution(mesh):
    placed = (
        P("lat", "lon", None, None),
        P("lat", "lon", None, None),
        P("lat", "lon", None),
        P(None, "lat", "lon", None),
    )
    return jax.shard_map(
        local,
        mesh=mesh,
        in_specs=placed,
        out_specs=(P("lat", "lon", None, None), P("lat", "lon", None, None)),
        check_vma=False,
    )
```

```python
import functools

import jax
import jax.numpy as jnp
from jax import lax
from jax.experimental import pallas as pl
from jax.experimental.pallas import tpu as pltpu
from jax.sharding import PartitionSpec as P

K = 80
COLS = 128
STRIDE = 16
RADIUS = 4
CODES = 9


def gaspari_cohn(shift_rows, shift_cols):
    position = jnp.arange(COLS)
    row_within = position // STRIDE
    col_within = position % STRIDE
    delta_rows = shift_rows[..., None, None] + (row_within[None, :] - row_within[:, None])
    delta_cols = shift_cols[..., None, None] + (col_within[None, :] - col_within[:, None])
    squared = (delta_rows * delta_rows + delta_cols * delta_cols).astype(jnp.float32)
    scaled = jnp.sqrt(squared + 0.25) / RADIUS
    inside = (
        ((-0.25 * scaled + 0.5) * scaled + 0.625) * scaled - 5.0 / 3.0
    ) * scaled * scaled + 1.0
    outside = (
        ((((scaled / 12.0 - 0.5) * scaled + 0.625) * scaled + 5.0 / 3.0) * scaled - 5.0) * scaled
        + 4.0
        - 2.0 / (3.0 * scaled)
    )
    return jnp.where(scaled <= 1.0, inside, jnp.where(scaled <= 2.0, outside, 0.0))


def taper_by_code():
    codes = jnp.arange(CODES, dtype=jnp.int32)
    shift_rows = (codes // 3 - 1) * (COLS // STRIDE)
    shift_cols = (codes % 3 - 1) * STRIDE
    return gaspari_cohn(shift_rows, shift_cols) / (K - 1)


def with_halo(cells):
    nlat = lax.axis_size("lat")
    nlon = lax.axis_size("lon")
    down = [(i, i + 1) for i in range(nlat - 1)]
    up = [(i + 1, i) for i in range(nlat - 1)]
    right = [(i, (i + 1) % nlon) for i in range(nlon)]
    left = [((i + 1) % nlon, i) for i in range(nlon)]

    def both(lat_pairs, lon_shift):
        return [
            (b * nlat + a, ((b + lon_shift) % nlon) * nlat + c)
            for a, c in lat_pairs
            for b in range(nlon)
        ]

    first_row, last_row = cells[:1], cells[-1:]
    north = lax.ppermute(last_row, "lat", down)
    south = lax.ppermute(first_row, "lat", up)
    west = lax.ppermute(cells[:, -1:], "lon", right)
    east = lax.ppermute(cells[:, :1], "lon", left)
    north_west = lax.ppermute(last_row[:, -1:], ("lon", "lat"), both(down, 1))
    north_east = lax.ppermute(last_row[:, :1], ("lon", "lat"), both(down, -1))
    south_west = lax.ppermute(first_row[:, -1:], ("lon", "lat"), both(up, 1))
    south_east = lax.ppermute(first_row[:, :1], ("lon", "lat"), both(up, -1))
    top = jnp.concatenate([north_west, north, north_east], axis=1)
    middle = jnp.concatenate([west, cells, east], axis=1)
    bottom = jnp.concatenate([south_west, south, south_east], axis=1)
    return jnp.concatenate([top, middle, bottom], axis=0)


def product_kernel(field_at, targets_ref, members_ref, field_ref, taper_ref, out_ref):
    lat_blocks, lon_blocks, columns, rank = out_ref.shape

    def one_block(t, carry):
        p = t // lon_blocks
        q = t % lon_blocks
        target = targets_ref[p, q]
        total = jnp.zeros((columns, rank), jnp.float32)
        for code in range(CODES):
            dr, dc = code // 3, code % 3
            gram = jnp.dot(
                target, members_ref[p + dr, q + dc, :K, :], preferred_element_type=jnp.float32
            )
            tile = gram * taper_ref[code]
            tile_high = tile.astype(jnp.bfloat16)
            tile_low = (tile - tile_high.astype(jnp.float32)).astype(jnp.bfloat16)
            field_high = field_ref[p + dr, q + dc, field_at : field_at + columns, :]
            field_low = field_ref[p + dr, q + dc, field_at + columns : field_at + 2 * columns, :]
            total = total + jnp.dot(tile_high, field_high, preferred_element_type=jnp.float32)
            total = total + jnp.dot(tile_high, field_low, preferred_element_type=jnp.float32)
            total = total + jnp.dot(tile_low, field_high, preferred_element_type=jnp.float32)
        out_ref[p, q] = total
        return carry

    lax.fori_loop(0, lat_blocks * lon_blocks, one_block, 0)


def split_high_low(field):
    rounded = lax.reduce_precision(field, exponent_bits=8, mantissa_bits=7)
    return rounded.astype(jnp.bfloat16), (field - rounded).astype(jnp.bfloat16)


def localized_product(targets, members_wide, field_wide, field_at, out_like):
    lat_blocks, lon_blocks, columns, rank = out_like.shape
    taper = taper_by_code()
    blocks = lat_blocks * lon_blocks
    flops = blocks * CODES * 2 * columns * (K * columns + 3 * columns * rank)
    moved = field_wide.size * 2 + members_wide.size * 2 + targets.size * 2 + taper.size * 4 + out_like.size * 4
    vmem = pl.BlockSpec(memory_space=pltpu.VMEM)
    return pl.pallas_call(
        functools.partial(product_kernel, field_at),
        out_shape=jax.ShapeDtypeStruct(out_like.shape, jnp.float32),
        in_specs=[vmem] * 4,
        out_specs=vmem,
        cost_estimate=pl.CostEstimate(flops=flops, bytes_accessed=moved, transcendentals=0),
    )(targets, members_wide, field_wide, taper)


def local(anomalies, panel, pair_code, pair_offset):
    del pair_code, pair_offset
    targets = jnp.swapaxes(anomalies, 2, 3)
    panel_high, panel_low = split_high_low(panel)
    first_wide = with_halo(jnp.concatenate([anomalies, panel_high, panel_low], axis=2))
    first_product = localized_product(targets, first_wide, first_wide, K, panel)
    product_high, product_low = split_high_low(first_product)
    second_wide = with_halo(jnp.concatenate([product_high, product_low], axis=2))
    second_product = localized_product(targets, first_wide, second_wide, 0, first_product)
    return (first_product, second_product)


def solution(mesh):
    placed = (
        P("lat", "lon", None, None),
        P("lat", "lon", None, None),
        P("lat", "lon", None),
        P(None, "lat", "lon", None),
    )
    return jax.shard_map(
        local,
        mesh=mesh,
        in_specs=placed,
        out_specs=(P("lat", "lon", None, None), P("lat", "lon", None, None)),
        check_vma=False,
    )
```

```python
import functools

import jax
import jax.numpy as jnp
from jax import lax
from jax.experimental import pallas as pl
from jax.experimental.pallas import tpu as pltpu
from jax.sharding import PartitionSpec as P

K = 80
COLS = 128
STRIDE = 16
RADIUS = 4
CODES = 9


def gaspari_cohn(shift_rows, shift_cols):
    position = jnp.arange(COLS)
    row_within = position // STRIDE
    col_within = position % STRIDE
    delta_rows = shift_rows[..., None, None] + (row_within[None, :] - row_within[:, None])
    delta_cols = shift_cols[..., None, None] + (col_within[None, :] - col_within[:, None])
    squared = (delta_rows * delta_rows + delta_cols * delta_cols).astype(jnp.float32)
    scaled = jnp.sqrt(squared + 0.25) / RADIUS
    inside = (
        ((-0.25 * scaled + 0.5) * scaled + 0.625) * scaled - 5.0 / 3.0
    ) * scaled * scaled + 1.0
    outside = (
        ((((scaled / 12.0 - 0.5) * scaled + 0.625) * scaled + 5.0 / 3.0) * scaled - 5.0) * scaled
        + 4.0
        - 2.0 / (3.0 * scaled)
    )
    return jnp.where(scaled <= 1.0, inside, jnp.where(scaled <= 2.0, outside, 0.0))


def taper_by_code():
    codes = jnp.arange(CODES, dtype=jnp.int32)
    shift_rows = (codes // 3 - 1) * (COLS // STRIDE)
    shift_cols = (codes % 3 - 1) * STRIDE
    return gaspari_cohn(shift_rows, shift_cols) / (K - 1)


def with_halo(cells):
    nlat = lax.axis_size("lat")
    nlon = lax.axis_size("lon")
    west = lax.ppermute(cells[:, -1:], "lon", [(i, (i + 1) % nlon) for i in range(nlon)])
    east = lax.ppermute(cells[:, :1], "lon", [((i + 1) % nlon, i) for i in range(nlon)])
    wider = jnp.concatenate([west, cells, east], axis=1)
    north = lax.ppermute(wider[-1:], "lat", [(i, i + 1) for i in range(nlat - 1)])
    south = lax.ppermute(wider[:1], "lat", [(i + 1, i) for i in range(nlat - 1)])
    return jnp.concatenate([north, wider, south], axis=0)


def product_kernel(field_at, targets_ref, members_ref, field_ref, taper_ref, out_ref):
    lat_blocks, lon_blocks, columns, rank = out_ref.shape

    def one_block(t, carry):
        p = t // lon_blocks
        q = t % lon_blocks
        target = targets_ref[p, q]
        total = jnp.zeros((columns, rank), jnp.float32)
        for code in range(CODES):
            dr, dc = code // 3, code % 3
            gram = jnp.dot(
                target, members_ref[p + dr, q + dc, :K, :], preferred_element_type=jnp.float32
            )
            tile = gram * taper_ref[code]
            tile_high = tile.astype(jnp.bfloat16)
            tile_low = (tile - tile_high.astype(jnp.float32)).astype(jnp.bfloat16)
            field_high = field_ref[p + dr, q + dc, field_at : field_at + columns, :]
            field_low = field_ref[p + dr, q + dc, field_at + columns : field_at + 2 * columns, :]
            total = total + jnp.dot(tile_high, field_high, preferred_element_type=jnp.float32)
            total = total + jnp.dot(tile_high, field_low, preferred_element_type=jnp.float32)
            total = total + jnp.dot(tile_low, field_high, preferred_element_type=jnp.float32)
        out_ref[p, q] = total
        return carry

    lax.fori_loop(0, lat_blocks * lon_blocks, one_block, 0)


def split_high_low(field):
    rounded = lax.reduce_precision(field, exponent_bits=8, mantissa_bits=7)
    return rounded.astype(jnp.bfloat16), (field - rounded).astype(jnp.bfloat16)


def localized_product(targets, members_wide, field_wide, field_at, out_like):
    lat_blocks, lon_blocks, columns, rank = out_like.shape
    taper = taper_by_code()
    blocks = lat_blocks * lon_blocks
    flops = blocks * CODES * 2 * columns * (K * columns + 3 * columns * rank)
    moved = field_wide.size * 2 + members_wide.size * 2 + targets.size * 2 + taper.size * 4 + out_like.size * 4
    vmem = pl.BlockSpec(memory_space=pltpu.VMEM)
    return pl.pallas_call(
        functools.partial(product_kernel, field_at),
        out_shape=jax.ShapeDtypeStruct(out_like.shape, jnp.float32),
        in_specs=[vmem] * 4,
        out_specs=vmem,
        cost_estimate=pl.CostEstimate(flops=flops, bytes_accessed=moved, transcendentals=0),
    )(targets, members_wide, field_wide, taper)


def local(anomalies, panel, pair_code, pair_offset):
    del pair_code, pair_offset
    targets = jnp.swapaxes(anomalies, 2, 3)
    panel_high, panel_low = split_high_low(panel)
    first_wide = with_halo(jnp.concatenate([anomalies, panel_high, panel_low], axis=2))
    first_product = localized_product(targets, first_wide, first_wide, K, panel)
    product_high, product_low = split_high_low(first_product)
    second_wide = with_halo(jnp.concatenate([product_high, product_low], axis=2))
    second_product = localized_product(targets, first_wide, second_wide, 0, first_product)
    return (first_product, second_product)


def solution(mesh):
    placed = (
        P("lat", "lon", None, None),
        P("lat", "lon", None, None),
        P("lat", "lon", None),
        P(None, "lat", "lon", None),
    )
    return jax.shard_map(
        local,
        mesh=mesh,
        in_specs=placed,
        out_specs=(P("lat", "lon", None, None), P("lat", "lon", None, None)),
        check_vma=False,
    )
```

```python
import functools

import jax
import jax.numpy as jnp
from jax import lax
from jax.experimental import pallas as pl
from jax.experimental.pallas import tpu as pltpu
from jax.sharding import PartitionSpec as P

K = 80
COLS = 128
STRIDE = 16
RADIUS = 4
CODES = 9


def gaspari_cohn(shift_rows, shift_cols):
    position = jnp.arange(COLS)
    row_within = position // STRIDE
    col_within = position % STRIDE
    delta_rows = shift_rows[..., None, None] + (row_within[None, :] - row_within[:, None])
    delta_cols = shift_cols[..., None, None] + (col_within[None, :] - col_within[:, None])
    squared = (delta_rows * delta_rows + delta_cols * delta_cols).astype(jnp.float32)
    scaled = jnp.sqrt(squared + 0.25) / RADIUS
    inside = (
        ((-0.25 * scaled + 0.5) * scaled + 0.625) * scaled - 5.0 / 3.0
    ) * scaled * scaled + 1.0
    outside = (
        ((((scaled / 12.0 - 0.5) * scaled + 0.625) * scaled + 5.0 / 3.0) * scaled - 5.0) * scaled
        + 4.0
        - 2.0 / (3.0 * scaled)
    )
    return jnp.where(scaled <= 1.0, inside, jnp.where(scaled <= 2.0, outside, 0.0))


def taper_by_code():
    codes = jnp.arange(CODES, dtype=jnp.int32)
    shift_rows = (codes // 3 - 1) * (COLS // STRIDE)
    shift_cols = (codes % 3 - 1) * STRIDE
    table = gaspari_cohn(shift_rows, shift_cols) / (K - 1)
    return table.reshape(3, 3 * COLS, COLS)


def with_halo(cells):
    nlat = lax.axis_size("lat")
    nlon = lax.axis_size("lon")
    west = lax.ppermute(cells[:, -1:], "lon", [(i, (i + 1) % nlon) for i in range(nlon)])
    east = lax.ppermute(cells[:, :1], "lon", [((i + 1) % nlon, i) for i in range(nlon)])
    wider = jnp.concatenate([west, cells, east], axis=1)
    north = lax.ppermute(wider[-1:], "lat", [(i, i + 1) for i in range(nlat - 1)])
    south = lax.ppermute(wider[:1], "lat", [(i + 1, i) for i in range(nlat - 1)])
    return jnp.concatenate([north, wider, south], axis=0)


def product_kernel(field_at, targets_ref, members_ref, field_ref, taper_ref, out_ref):
    lat_blocks, lon_blocks, columns, rank = out_ref.shape
    out_ref[...] = jnp.zeros(out_ref.shape, jnp.float32)
    for p in range(lat_blocks):
        for dr in range(3):
            row = p + dr

            def step(c, carry, p=p, dr=dr, row=row):
                lhs = jnp.concatenate(
                    [targets_ref[p, jnp.clip(c - k, 0, lon_blocks - 1)] for k in range(3)], axis=0
                )
                gram = jnp.dot(lhs, members_ref[row, c, :K, :], preferred_element_type=jnp.float32)
                tile = gram * taper_ref[dr]
                high = tile.astype(jnp.bfloat16)
                low = (tile - high.astype(jnp.float32)).astype(jnp.bfloat16)
                field_high = field_ref[row, c, field_at : field_at + columns, :]
                field_low = field_ref[row, c, field_at + columns : field_at + 2 * columns, :]
                both = jnp.dot(
                    jnp.concatenate([high, low], axis=0), field_high, preferred_element_type=jnp.float32
                )
                cross = jnp.dot(high, field_low, preferred_element_type=jnp.float32)
                for k in range(3):
                    q = c - k
                    part = (
                        both[k * columns : (k + 1) * columns]
                        + both[(3 + k) * columns : (4 + k) * columns]
                        + cross[k * columns : (k + 1) * columns]
                    )

                    @pl.when((q >= 0) & (q < lon_blocks))
                    def _(q=q, part=part):
                        at = jnp.clip(q, 0, lon_blocks - 1)
                        out_ref[p, at] = out_ref[p, at] + part

                return carry

            lax.fori_loop(0, lon_blocks + 2, step, 0)


def split_high_low(field):
    rounded = lax.reduce_precision(field, exponent_bits=8, mantissa_bits=7)
    return rounded.astype(jnp.bfloat16), (field - rounded).astype(jnp.bfloat16)


def localized_product(targets, members_wide, field_wide, field_at, out_like):
    lat_blocks, lon_blocks, columns, rank = out_like.shape
    taper = taper_by_code()
    blocks = lat_blocks * lon_blocks
    flops = blocks * CODES * 2 * columns * (K * columns + 3 * columns * rank)
    moved = field_wide.size * 2 + members_wide.size * 2 + targets.size * 2 + taper.size * 4 + out_like.size * 4
    vmem = pl.BlockSpec(memory_space=pltpu.VMEM)
    return pl.pallas_call(
        functools.partial(product_kernel, field_at),
        out_shape=jax.ShapeDtypeStruct(out_like.shape, jnp.float32),
        in_specs=[vmem] * 4,
        out_specs=vmem,
        cost_estimate=pl.CostEstimate(flops=flops, bytes_accessed=moved, transcendentals=0),
    )(targets, members_wide, field_wide, taper)


def local(anomalies, panel, pair_code, pair_offset):
    del pair_code, pair_offset
    targets = jnp.swapaxes(anomalies, 2, 3)
    panel_high, panel_low = split_high_low(panel)
    first_wide = with_halo(jnp.concatenate([anomalies, panel_high, panel_low], axis=2))
    first_product = localized_product(targets, first_wide, first_wide, K, panel)
    product_high, product_low = split_high_low(first_product)
    second_wide = with_halo(jnp.concatenate([product_high, product_low], axis=2))
    second_product = localized_product(targets, first_wide, second_wide, 0, first_product)
    return (first_product, second_product)


def solution(mesh):
    placed = (
        P("lat", "lon", None, None),
        P("lat", "lon", None, None),
        P("lat", "lon", None),
        P(None, "lat", "lon", None),
    )
    return jax.shard_map(
        local,
        mesh=mesh,
        in_specs=placed,
        out_specs=(P("lat", "lon", None, None), P("lat", "lon", None, None)),
        check_vma=False,
    )
```

```python
import functools

import jax
import jax.numpy as jnp
from jax import lax
from jax.experimental import pallas as pl
from jax.experimental.pallas import tpu as pltpu
from jax.sharding import PartitionSpec as P

K = 80
COLS = 128
STRIDE = 16
RADIUS = 4
CODES = 9


def gaspari_cohn(shift_rows, shift_cols):
    position = jnp.arange(COLS)
    row_within = position // STRIDE
    col_within = position % STRIDE
    delta_rows = shift_rows[..., None, None] + (row_within[None, :] - row_within[:, None])
    delta_cols = shift_cols[..., None, None] + (col_within[None, :] - col_within[:, None])
    squared = (delta_rows * delta_rows + delta_cols * delta_cols).astype(jnp.float32)
    scaled = jnp.sqrt(squared + 0.25) / RADIUS
    inside = (
        ((-0.25 * scaled + 0.5) * scaled + 0.625) * scaled - 5.0 / 3.0
    ) * scaled * scaled + 1.0
    outside = (
        ((((scaled / 12.0 - 0.5) * scaled + 0.625) * scaled + 5.0 / 3.0) * scaled - 5.0) * scaled
        + 4.0
        - 2.0 / (3.0 * scaled)
    )
    return jnp.where(scaled <= 1.0, inside, jnp.where(scaled <= 2.0, outside, 0.0))


def taper_by_code():
    codes = jnp.arange(CODES, dtype=jnp.int32)
    shift_rows = (codes // 3 - 1) * (COLS // STRIDE)
    shift_cols = (codes % 3 - 1) * STRIDE
    return gaspari_cohn(shift_rows, shift_cols) / (K - 1)


def with_halo(cells):
    nlat = lax.axis_size("lat")
    nlon = lax.axis_size("lon")
    west = lax.ppermute(cells[:, -1:], "lon", [(i, (i + 1) % nlon) for i in range(nlon)])
    east = lax.ppermute(cells[:, :1], "lon", [((i + 1) % nlon, i) for i in range(nlon)])
    wider = jnp.concatenate([west, cells, east], axis=1)
    north = lax.ppermute(wider[-1:], "lat", [(i, i + 1) for i in range(nlat - 1)])
    south = lax.ppermute(wider[:1], "lat", [(i + 1, i) for i in range(nlat - 1)])
    return north, wider, south


def rows_kernel(plan, field_at, with_partial, targets_ref, taper_ref, *rest):
    out_ref = rest[-1]
    partial_ref = rest[0] if with_partial else None
    sources = rest[1:-1] if with_partial else rest[:-1]
    lat_blocks, lon_blocks, columns, rank = out_ref.shape
    for p in range(lat_blocks):

        def one_block(q, carry, p=p, uses=plan[p]):
            target = targets_ref[p, q]
            if with_partial:
                total = partial_ref[p, q]
            else:
                total = jnp.zeros((columns, rank), jnp.float32)
            for dr, members_at, field_from, row in uses:
                members_ref, field_ref = sources[members_at], sources[field_from]
                for dc in range(3):
                    gram = jnp.dot(
                        target, members_ref[row, q + dc, :K, :], preferred_element_type=jnp.float32
                    )
                    tile = gram * taper_ref[dr * 3 + dc]
                    tile_high = tile.astype(jnp.bfloat16)
                    tile_low = (tile - tile_high.astype(jnp.float32)).astype(jnp.bfloat16)
                    field_high = field_ref[row, q + dc, field_at : field_at + columns, :]
                    field_low = field_ref[row, q + dc, field_at + columns : field_at + 2 * columns, :]
                    total = total + jnp.dot(tile_high, field_high, preferred_element_type=jnp.float32)
                    total = total + jnp.dot(tile_high, field_low, preferred_element_type=jnp.float32)
                    total = total + jnp.dot(tile_low, field_high, preferred_element_type=jnp.float32)
            out_ref[p, q] = total
            return carry

        lax.fori_loop(0, lon_blocks, one_block, 0)


def rows_call(plan, field_at, targets, taper, partial, sources, out_like):
    lat_blocks, lon_blocks, columns, rank = out_like.shape
    codes = sum(3 * len(uses) for uses in plan)
    flops = lon_blocks * codes * 2 * columns * (K * columns + 3 * columns * rank)
    operands = [targets, taper] + ([partial] if partial is not None else []) + list(sources)
    moved = sum(x.size * x.dtype.itemsize for x in operands) + out_like.size * 4
    vmem = pl.BlockSpec(memory_space=pltpu.VMEM)
    return pl.pallas_call(
        functools.partial(rows_kernel, plan, field_at, partial is not None),
        out_shape=jax.ShapeDtypeStruct(out_like.shape, jnp.float32),
        in_specs=[vmem] * len(operands),
        out_specs=vmem,
        cost_estimate=pl.CostEstimate(flops=flops, bytes_accessed=moved, transcendentals=0),
    )(*operands)


def split_high_low(field):
    rounded = lax.reduce_precision(field, exponent_bits=8, mantissa_bits=7)
    return rounded.astype(jnp.bfloat16), (field - rounded).astype(jnp.bfloat16)


def own_plan(lat_blocks, members, field):
    return tuple(
        tuple((dr, members, field, p + dr - 1) for dr in range(3) if 0 <= p + dr - 1 < lat_blocks)
        for p in range(lat_blocks)
    )


def halo_plan(lat_blocks, members, field):
    return tuple(
        tuple(
            (dr, members[p + dr > 0], field[p + dr > 0], 0)
            for dr in range(3)
            if not 0 <= p + dr - 1 < lat_blocks
        )
        for p in range(lat_blocks)
    )


def local(anomalies, panel, pair_code, pair_offset):
    del pair_code, pair_offset
    lat_blocks = anomalies.shape[0]
    taper = taper_by_code()
    targets = jnp.swapaxes(anomalies, 2, 3)
    panel_high, panel_low = split_high_low(panel)
    north, wider, south = with_halo(jnp.concatenate([anomalies, panel_high, panel_low], axis=2))
    partial = rows_call(own_plan(lat_blocks, 0, 0), K, targets, taper, None, (wider,), panel)
    first_product = rows_call(
        halo_plan(lat_blocks, (0, 1), (0, 1)), K, targets, taper, partial, (north, south), panel
    )
    product_high, product_low = split_high_low(first_product)
    north2, wider2, south2 = with_halo(jnp.concatenate([product_high, product_low], axis=2))
    partial = rows_call(own_plan(lat_blocks, 0, 1), 0, targets, taper, None, (wider, wider2), panel)
    second_product = rows_call(
        halo_plan(lat_blocks, (0, 1), (2, 3)),
        0,
        targets,
        taper,
        partial,
        (north, south, north2, south2),
        panel,
    )
    return (first_product, second_product)


def solution(mesh):
    placed = (
        P("lat", "lon", None, None),
        P("lat", "lon", None, None),
        P("lat", "lon", None),
        P(None, "lat", "lon", None),
    )
    return jax.shard_map(
        local,
        mesh=mesh,
        in_specs=placed,
        out_specs=(P("lat", "lon", None, None), P("lat", "lon", None, None)),
        check_vma=False,
    )
```

```python
import functools

import jax
import jax.numpy as jnp
from jax import lax
from jax.experimental import pallas as pl
from jax.experimental.pallas import tpu as pltpu
from jax.sharding import PartitionSpec as P

K = 80
COLS = 128
STRIDE = 16
RADIUS = 4
CODES = 9


def gaspari_cohn(shift_rows, shift_cols):
    position = jnp.arange(COLS)
    row_within = position // STRIDE
    col_within = position % STRIDE
    delta_rows = shift_rows[..., None, None] + (row_within[None, :] - row_within[:, None])
    delta_cols = shift_cols[..., None, None] + (col_within[None, :] - col_within[:, None])
    squared = (delta_rows * delta_rows + delta_cols * delta_cols).astype(jnp.float32)
    scaled = jnp.sqrt(squared + 0.25) / RADIUS
    inside = (
        ((-0.25 * scaled + 0.5) * scaled + 0.625) * scaled - 5.0 / 3.0
    ) * scaled * scaled + 1.0
    outside = (
        ((((scaled / 12.0 - 0.5) * scaled + 0.625) * scaled + 5.0 / 3.0) * scaled - 5.0) * scaled
        + 4.0
        - 2.0 / (3.0 * scaled)
    )
    return jnp.where(scaled <= 1.0, inside, jnp.where(scaled <= 2.0, outside, 0.0))


def taper_by_code():
    codes = jnp.arange(CODES, dtype=jnp.int32)
    shift_rows = (codes // 3 - 1) * (COLS // STRIDE)
    shift_cols = (codes % 3 - 1) * STRIDE
    return gaspari_cohn(shift_rows, shift_cols) / (K - 1)


def lon_halo(cells, depth):
    nlon = lax.axis_size("lon")
    west = lax.ppermute(cells[:, -depth:], "lon", [(i, (i + 1) % nlon) for i in range(nlon)])
    east = lax.ppermute(cells[:, :depth], "lon", [((i + 1) % nlon, i) for i in range(nlon)])
    return jnp.concatenate([west, cells, east], axis=1)


def lat_halo(rows):
    nlat = lax.axis_size("lat")
    north = lax.ppermute(rows[-1:], "lat", [(i, i + 1) for i in range(nlat - 1)])
    south = lax.ppermute(rows[:1], "lat", [(i + 1, i) for i in range(nlat - 1)])
    return north, south


def rows_kernel(plan, field_at, with_partial, targets_ref, taper_ref, *rest):
    out_ref = rest[-1]
    partial_ref = rest[0] if with_partial else None
    sources = rest[1:-1] if with_partial else rest[:-1]
    lat_blocks, lon_blocks, columns, rank = out_ref.shape
    for p in range(lat_blocks):

        def one_block(q, carry, p=p, uses=plan[p]):
            target = targets_ref[p, q]
            if with_partial:
                total = partial_ref[p, q]
            else:
                total = jnp.zeros((columns, rank), jnp.float32)
            for dr, members_at, field_from, row, members_off, field_off in uses:
                members_ref, field_ref = sources[members_at], sources[field_from]
                for dc in range(3):
                    gram = jnp.dot(
                        target,
                        members_ref[row, q + dc + members_off, :K, :],
                        preferred_element_type=jnp.float32,
                    )
                    tile = gram * taper_ref[dr * 3 + dc]
                    tile_high = tile.astype(jnp.bfloat16)
                    tile_low = (tile - tile_high.astype(jnp.float32)).astype(jnp.bfloat16)
                    partner = field_ref.at[row, q + dc + field_off]
                    field_high = partner[field_at : field_at + columns, :]
                    field_low = partner[field_at + columns : field_at + 2 * columns, :]
                    total = total + jnp.dot(tile_high, field_high, preferred_element_type=jnp.float32)
                    total = total + jnp.dot(tile_high, field_low, preferred_element_type=jnp.float32)
                    total = total + jnp.dot(tile_low, field_high, preferred_element_type=jnp.float32)
            out_ref[p, q] = total
            return carry

        lax.fori_loop(0, lon_blocks, one_block, 0)


def rows_call(plan, field_at, targets, taper, partial, sources, out_like):
    lat_blocks, lon_blocks, columns, rank = out_like.shape
    codes = sum(3 * len(uses) for uses in plan)
    flops = lon_blocks * codes * 2 * columns * (K * columns + 3 * columns * rank)
    operands = [targets, taper] + ([partial] if partial is not None else []) + list(sources)
    moved = sum(x.size * x.dtype.itemsize for x in operands) + out_like.size * 4
    vmem = pl.BlockSpec(memory_space=pltpu.VMEM)
    return pl.pallas_call(
        functools.partial(rows_kernel, plan, field_at, partial is not None),
        out_shape=jax.ShapeDtypeStruct(out_like.shape, jnp.float32),
        in_specs=[vmem] * len(operands),
        out_specs=vmem,
        cost_estimate=pl.CostEstimate(flops=flops, bytes_accessed=moved, transcendentals=0),
    )(*operands)


def split_high_low(field):
    rounded = lax.reduce_precision(field, exponent_bits=8, mantissa_bits=7)
    return rounded.astype(jnp.bfloat16), (field - rounded).astype(jnp.bfloat16)


def own_plan(lat_blocks, members, field, offsets):
    return tuple(
        tuple((dr, members, field, p + dr - 1) + offsets for dr in range(3) if 0 <= p + dr - 1 < lat_blocks)
        for p in range(lat_blocks)
    )


def halo_plan(lat_blocks, members, field, offsets):
    return tuple(
        tuple(
            (dr, members[p + dr > 0], field[p + dr > 0], 0) + offsets
            for dr in range(3)
            if not 0 <= p + dr - 1 < lat_blocks
        )
        for p in range(lat_blocks)
    )


def local(anomalies, panel, pair_code, pair_offset):
    del pair_code, pair_offset
    lat_blocks, lon_blocks = anomalies.shape[:2]
    taper = taper_by_code()
    panel_high, panel_low = split_high_low(panel)
    wider = lon_halo(jnp.concatenate([anomalies, panel_high, panel_low], axis=2), 2)
    north, south = lat_halo(wider)
    targets_wide = jnp.swapaxes(wider[:, 1 : lon_blocks + 3, :K, :], 2, 3)
    like_wide = jax.ShapeDtypeStruct((lat_blocks, lon_blocks + 2) + panel.shape[2:], jnp.float32)
    partial = rows_call(own_plan(lat_blocks, 0, 0, (0, 0)), K, targets_wide, taper, None, (wider,), like_wide)
    product_wide = rows_call(
        halo_plan(lat_blocks, (0, 1), (0, 1), (0, 0)), K, targets_wide, taper, partial, (north, south), like_wide
    )
    first_product = product_wide[:, 1 : lon_blocks + 1]
    product_high, product_low = split_high_low(product_wide)
    message = jnp.concatenate([product_high, product_low], axis=2)
    north2, south2 = lat_halo(message)
    targets = jnp.swapaxes(anomalies, 2, 3)
    partial = rows_call(own_plan(lat_blocks, 0, 1, (1, 0)), 0, targets, taper, None, (wider, message), panel)
    second_product = rows_call(
        halo_plan(lat_blocks, (0, 1), (2, 3), (1, 0)),
        0,
        targets,
        taper,
        partial,
        (north, south, north2, south2),
        panel,
    )
    return (first_product, second_product)


def solution(mesh):
    placed = (
        P("lat", "lon", None, None),
        P("lat", "lon", None, None),
        P("lat", "lon", None),
        P(None, "lat", "lon", None),
    )
    return jax.shard_map(
        local,
        mesh=mesh,
        in_specs=placed,
        out_specs=(P("lat", "lon", None, None), P("lat", "lon", None, None)),
        check_vma=False,
    )
```

```python
import functools

import jax
import jax.numpy as jnp
from jax import lax
from jax.experimental import pallas as pl
from jax.experimental.pallas import tpu as pltpu
from jax.sharding import PartitionSpec as P

K = 80
COLS = 128
STRIDE = 16
RADIUS = 4
CODES = 9


def gaspari_cohn(shift_rows, shift_cols):
    position = jnp.arange(COLS)
    row_within = position // STRIDE
    col_within = position % STRIDE
    delta_rows = shift_rows[..., None, None] + (row_within[None, :] - row_within[:, None])
    delta_cols = shift_cols[..., None, None] + (col_within[None, :] - col_within[:, None])
    squared = (delta_rows * delta_rows + delta_cols * delta_cols).astype(jnp.float32)
    scaled = jnp.sqrt(squared + 0.25) / RADIUS
    inside = (
        ((-0.25 * scaled + 0.5) * scaled + 0.625) * scaled - 5.0 / 3.0
    ) * scaled * scaled + 1.0
    outside = (
        ((((scaled / 12.0 - 0.5) * scaled + 0.625) * scaled + 5.0 / 3.0) * scaled - 5.0) * scaled
        + 4.0
        - 2.0 / (3.0 * scaled)
    )
    return jnp.where(scaled <= 1.0, inside, jnp.where(scaled <= 2.0, outside, 0.0))


def taper_by_code():
    codes = jnp.arange(CODES, dtype=jnp.int32)
    shift_rows = (codes // 3 - 1) * (COLS // STRIDE)
    shift_cols = (codes % 3 - 1) * STRIDE
    return gaspari_cohn(shift_rows, shift_cols) / (K - 1)


def lon_halo(cells, depth):
    nlon = lax.axis_size("lon")
    west = lax.ppermute(cells[:, -depth:], "lon", [(i, (i + 1) % nlon) for i in range(nlon)])
    east = lax.ppermute(cells[:, :depth], "lon", [((i + 1) % nlon, i) for i in range(nlon)])
    return jnp.concatenate([west, cells, east], axis=1)


def lat_halo(first_row, last_row):
    nlat = lax.axis_size("lat")
    north = lax.ppermute(last_row, "lat", [(i, i + 1) for i in range(nlat - 1)])
    south = lax.ppermute(first_row, "lat", [(i + 1, i) for i in range(nlat - 1)])
    return north, south


def rows_kernel(plan, field_at, with_partial, target_off, emit, targets_ref, taper_ref, *rest):
    outs = rest[-(1 + len(emit)) :] if emit else rest[-1:]
    rest = rest[: len(rest) - len(outs)]
    out_ref = outs[0]
    partial_ref = rest[0] if with_partial else None
    sources = rest[1:] if with_partial else rest
    columns, rank = out_ref.shape[2:]
    lat_blocks = out_ref.shape[0]
    lon_blocks = partial_ref.shape[1] if emit else out_ref.shape[1]
    for p in range(lat_blocks):

        def one_block(q, carry, p=p, uses=plan[p]):
            target = targets_ref[p, q + target_off]
            if with_partial:
                total = partial_ref[p, q]
            else:
                total = jnp.zeros((columns, rank), jnp.float32)
            for dr, members_at, members_row, field_from, row, members_off, field_off in uses:
                members_ref, field_ref = sources[members_at], sources[field_from]
                for dc in range(3):
                    gram = jnp.dot(
                        target,
                        members_ref[members_row, q + dc + members_off, :K, :],
                        preferred_element_type=jnp.float32,
                    )
                    tile = gram * taper_ref[dr * 3 + dc]
                    tile_high = tile.astype(jnp.bfloat16)
                    tile_low = (tile - tile_high.astype(jnp.float32)).astype(jnp.bfloat16)
                    partner = field_ref.at[row, q + dc + field_off]
                    field_high = partner[field_at : field_at + columns, :]
                    field_low = partner[field_at + columns : field_at + 2 * columns, :]
                    total = total + jnp.dot(tile_high, field_high, preferred_element_type=jnp.float32)
                    total = total + jnp.dot(tile_high, field_low, preferred_element_type=jnp.float32)
                    total = total + jnp.dot(tile_low, field_high, preferred_element_type=jnp.float32)
            if emit:
                inner = out_ref.shape[1]
                shift = (lon_blocks - inner) // 2

                @pl.when((q >= shift) & (q < shift + inner))
                def _():
                    out_ref[p, jnp.clip(q - shift, 0, inner - 1)] = total

                high = total.astype(jnp.bfloat16)
                low = (total - high.astype(jnp.float32)).astype(jnp.bfloat16)
                row_ref = outs[1 + emit[p]]
                row_ref[0, q, :columns, :] = high
                row_ref[0, q, columns:, :] = low
            else:
                out_ref[p, q] = total
            return carry

        lax.fori_loop(0, lon_blocks, one_block, 0)


def rows_call(plan, field_at, targets, taper, partial, sources, out_like, target_off=0, emit=()):
    lat_blocks, lon_blocks, columns, rank = (partial if emit else out_like).shape
    codes = sum(3 * len(uses) for uses in plan)
    flops = lon_blocks * codes * 2 * columns * (K * columns + 3 * columns * rank)
    operands = [targets, taper] + ([partial] if partial is not None else []) + list(sources)
    shapes = [jax.ShapeDtypeStruct(out_like.shape, jnp.float32)]
    if emit:
        shapes += [jax.ShapeDtypeStruct((1, lon_blocks, 2 * columns, rank), jnp.bfloat16)] * len(emit)
    moved = sum(x.size * x.dtype.itemsize for x in operands + shapes)
    vmem = pl.BlockSpec(memory_space=pltpu.VMEM)
    result = pl.pallas_call(
        functools.partial(rows_kernel, plan, field_at, partial is not None, target_off, emit),
        out_shape=tuple(shapes) if emit else shapes[0],
        in_specs=[vmem] * len(operands),
        out_specs=tuple([vmem] * len(shapes)) if emit else vmem,
        cost_estimate=pl.CostEstimate(flops=flops, bytes_accessed=moved, transcendentals=0),
    )(*operands)
    return result


def split_high_low(field):
    rounded = lax.reduce_precision(field, exponent_bits=8, mantissa_bits=7)
    return rounded.astype(jnp.bfloat16), (field - rounded).astype(jnp.bfloat16)


def own_plan(lat_blocks, members, fields, offsets):
    return tuple(
        tuple(
            (dr, members, p + dr - 1, fields[p + dr - 1], p + dr - 1 if len(set(fields)) == 1 else 0)
            + offsets
            for dr in range(3)
            if 0 <= p + dr - 1 < lat_blocks
        )
        for p in range(lat_blocks)
    )


def halo_plan(lat_blocks, members, field, offsets):
    return tuple(
        tuple(
            (dr, members[p + dr > 0], 0, field[p + dr > 0], 0) + offsets
            for dr in range(3)
            if not 0 <= p + dr - 1 < lat_blocks
        )
        for p in range(lat_blocks)
    )


def local(anomalies, panel, pair_code, pair_offset):
    del pair_code, pair_offset
    lat_blocks, lon_blocks = anomalies.shape[:2]
    taper = taper_by_code()
    panel_high, panel_low = split_high_low(panel)
    wider = lon_halo(jnp.concatenate([anomalies, panel_high, panel_low], axis=2), 2)
    north, south = lat_halo(wider[:1], wider[-1:])
    targets_wide = jnp.swapaxes(wider[:, 1 : lon_blocks + 3, :K, :], 2, 3)
    like_wide = jax.ShapeDtypeStruct((lat_blocks, lon_blocks + 2) + panel.shape[2:], jnp.float32)
    own_fields = (0,) * lat_blocks
    partial = rows_call(own_plan(lat_blocks, 0, own_fields, (0, 0)), K, targets_wide, taper, None, (wider,), like_wide)
    emit = tuple(0 if p == 0 else 1 for p in range(lat_blocks))
    first_product, first_row, last_row = rows_call(
        halo_plan(lat_blocks, (0, 1), (0, 1), (0, 0)),
        K,
        targets_wide,
        taper,
        partial,
        (north, south),
        panel,
        emit=emit,
    )
    north2, south2 = lat_halo(first_row, last_row)
    row_fields = (1, 2) if lat_blocks == 2 else None
    partial = rows_call(
        own_plan(lat_blocks, 0, row_fields, (1, 0)),
        0,
        targets_wide,
        taper,
        None,
        (wider, first_row, last_row),
        panel,
        target_off=1,
    )
    second_product = rows_call(
        halo_plan(lat_blocks, (0, 1), (2, 3), (1, 0)),
        0,
        targets_wide,
        taper,
        partial,
        (north, south, north2, south2),
        panel,
        target_off=1,
    )
    return (first_product, second_product)


def solution(mesh):
    placed = (
        P("lat", "lon", None, None),
        P("lat", "lon", None, None),
        P("lat", "lon", None),
        P(None, "lat", "lon", None),
    )
    return jax.shard_map(
        local,
        mesh=mesh,
        in_specs=placed,
        out_specs=(P("lat", "lon", None, None), P("lat", "lon", None, None)),
        check_vma=False,
    )
```

```python
import functools

import numpy as np

import jax
import jax.numpy as jnp
from jax import lax
from jax.experimental import pallas as pl
from jax.experimental.pallas import tpu as pltpu
from jax.sharding import PartitionSpec as P

K = 80
COLS = 128
STRIDE = 16
RADIUS = 4
CODES = 9


def taper_by_code():
    codes = np.arange(CODES)
    shift_rows = ((codes // 3 - 1) * (COLS // STRIDE))[:, None, None]
    shift_cols = ((codes % 3 - 1) * STRIDE)[:, None, None]
    position = np.arange(COLS)
    row_within = position // STRIDE
    col_within = position % STRIDE
    delta_rows = shift_rows + (row_within[None, :] - row_within[:, None])
    delta_cols = shift_cols + (col_within[None, :] - col_within[:, None])
    squared = (delta_rows * delta_rows + delta_cols * delta_cols).astype(np.float32)
    f = np.float32
    scaled = np.sqrt(squared + f(0.25)) / f(RADIUS)
    inside = (
        ((f(-0.25) * scaled + f(0.5)) * scaled + f(0.625)) * scaled - f(5.0 / 3.0)
    ) * scaled * scaled + f(1.0)
    outside = (
        ((((scaled / f(12.0) - f(0.5)) * scaled + f(0.625)) * scaled + f(5.0 / 3.0)) * scaled - f(5.0)) * scaled
        + f(4.0)
        - f(2.0) / (f(3.0) * scaled)
    )
    table = np.where(scaled <= 1.0, inside, np.where(scaled <= 2.0, outside, f(0.0))).astype(np.float32)
    return jnp.asarray(table / f(K - 1))


def lon_halo(cells, depth):
    nlon = lax.axis_size("lon")
    west = lax.ppermute(cells[:, -depth:], "lon", [(i, (i + 1) % nlon) for i in range(nlon)])
    east = lax.ppermute(cells[:, :depth], "lon", [((i + 1) % nlon, i) for i in range(nlon)])
    return jnp.concatenate([west, cells, east], axis=1), west, east


def lat_halo(first_row, last_row):
    nlat = lax.axis_size("lat")
    north = lax.ppermute(last_row, "lat", [(i, i + 1) for i in range(nlat - 1)])
    south = lax.ppermute(first_row, "lat", [(i + 1, i) for i in range(nlat - 1)])
    return north, south


def rows_kernel(plan, field_at, with_partial, target_off, emit, targets_ref, edges_ref, taper_ref, *rest):
    outs = rest[-(1 + len(emit)) :] if emit else rest[-1:]
    rest = rest[: len(rest) - len(outs)]
    out_ref = outs[0]
    partial_ref = rest[0] if with_partial else None
    sources = rest[1:] if with_partial else rest
    columns, rank = out_ref.shape[2:]
    lat_blocks = out_ref.shape[0]
    lon_blocks = partial_ref.shape[1] if emit else out_ref.shape[1]
    for p in range(lat_blocks):

        def one_block(q, carry, p=p, uses=plan[p], side=None):
            if side is None:
                target = targets_ref[p, q + target_off]
            else:
                target = edges_ref[p, side]
            if with_partial:
                total = partial_ref[p, q]
            else:
                total = jnp.zeros((columns, rank), jnp.float32)
            for dr, members_at, members_row, field_from, row, members_off, field_off in uses:
                members_ref, field_ref = sources[members_at], sources[field_from]
                for dc in range(3):
                    gram = jnp.dot(
                        target,
                        members_ref[members_row, q + dc + members_off, :K, :],
                        preferred_element_type=jnp.float32,
                    )
                    tile = gram * taper_ref[dr * 3 + dc]
                    tile_high = tile.astype(jnp.bfloat16)
                    tile_low = (tile - tile_high.astype(jnp.float32)).astype(jnp.bfloat16)
                    partner = field_ref.at[row, q + dc + field_off]
                    field_high = partner[field_at : field_at + columns, :]
                    field_low = partner[field_at + columns : field_at + 2 * columns, :]
                    total = total + jnp.dot(tile_high, field_high, preferred_element_type=jnp.float32)
                    total = total + jnp.dot(tile_high, field_low, preferred_element_type=jnp.float32)
                    total = total + jnp.dot(tile_low, field_high, preferred_element_type=jnp.float32)
            if emit:
                inner = out_ref.shape[1]
                shift = (lon_blocks - inner) // 2

                @pl.when((q >= shift) & (q < shift + inner))
                def _():
                    out_ref[p, jnp.clip(q - shift, 0, inner - 1)] = total

                high = total.astype(jnp.bfloat16)
                low = (total - high.astype(jnp.float32)).astype(jnp.bfloat16)
                row_ref = outs[1 + emit[p]]
                row_ref[0, q, :columns, :] = high
                row_ref[0, q, columns:, :] = low
            else:
                out_ref[p, q] = total
            return carry

        if edges_ref is None:
            lax.fori_loop(0, lon_blocks, one_block, 0)
        else:
            one_block(0, 0, side=0)
            lax.fori_loop(1, lon_blocks - 1, one_block, 0)
            one_block(lon_blocks - 1, 0, side=1)


def kernel_with_edges(*args):
    return rows_kernel(*args)


def kernel_without_edges(plan, field_at, with_partial, target_off, emit, targets_ref, *rest):
    return rows_kernel(plan, field_at, with_partial, target_off, emit, targets_ref, None, *rest)


def rows_call(plan, field_at, targets, taper, partial, sources, out_like, target_off=0, emit=(), edges=None):
    lat_blocks, lon_blocks, columns, rank = (partial if emit else out_like).shape
    codes = sum(3 * len(uses) for uses in plan)
    flops = lon_blocks * codes * 2 * columns * (K * columns + 3 * columns * rank)
    operands = [targets] + ([edges] if edges is not None else []) + [taper]
    operands += ([partial] if partial is not None else []) + list(sources)
    shapes = [jax.ShapeDtypeStruct(out_like.shape, jnp.float32)]
    if emit:
        shapes += [jax.ShapeDtypeStruct((1, lon_blocks, 2 * columns, rank), jnp.bfloat16)] * len(emit)
    moved = sum(x.size * x.dtype.itemsize for x in operands + shapes)
    vmem = pl.BlockSpec(memory_space=pltpu.VMEM)
    result = pl.pallas_call(
        functools.partial(
            kernel_with_edges if edges is not None else kernel_without_edges,
            plan,
            field_at,
            partial is not None,
            target_off,
            emit,
        ),
        out_shape=tuple(shapes) if emit else shapes[0],
        in_specs=[vmem] * len(operands),
        out_specs=tuple([vmem] * len(shapes)) if emit else vmem,
        cost_estimate=pl.CostEstimate(flops=flops, bytes_accessed=moved, transcendentals=0),
    )(*operands)
    return result


def split_high_low(field):
    rounded = lax.reduce_precision(field, exponent_bits=8, mantissa_bits=7)
    return rounded.astype(jnp.bfloat16), (field - rounded).astype(jnp.bfloat16)


def own_plan(lat_blocks, members, fields, offsets):
    return tuple(
        tuple(
            (dr, members, p + dr - 1, fields[p + dr - 1], p + dr - 1 if len(set(fields)) == 1 else 0)
            + offsets
            for dr in range(3)
            if 0 <= p + dr - 1 < lat_blocks
        )
        for p in range(lat_blocks)
    )


def halo_plan(lat_blocks, members, field, offsets):
    return tuple(
        tuple(
            (dr, members[p + dr > 0], 0, field[p + dr > 0], 0) + offsets
            for dr in range(3)
            if not 0 <= p + dr - 1 < lat_blocks
        )
        for p in range(lat_blocks)
    )


def local(anomalies, panel, pair_code, pair_offset):
    del pair_code, pair_offset
    lat_blocks, lon_blocks = anomalies.shape[:2]
    taper = taper_by_code()
    panel_high, panel_low = split_high_low(panel)
    wider, west, east = lon_halo(jnp.concatenate([anomalies, panel_high, panel_low], axis=2), 2)
    north, south = lat_halo(wider[:1], wider[-1:])
    targets = jnp.swapaxes(anomalies, 2, 3)
    edges = jnp.swapaxes(jnp.concatenate([west[:, 1:, :K, :], east[:, :1, :K, :]], axis=1), 2, 3)
    like_wide = jax.ShapeDtypeStruct((lat_blocks, lon_blocks + 2) + panel.shape[2:], jnp.float32)
    own_fields = (0,) * lat_blocks
    partial = rows_call(
        own_plan(lat_blocks, 0, own_fields, (0, 0)),
        K,
        targets,
        taper,
        None,
        (wider,),
        like_wide,
        target_off=-1,
        edges=edges,
    )
    emit = tuple(0 if p == 0 else 1 for p in range(lat_blocks))
    first_product, first_row, last_row = rows_call(
        halo_plan(lat_blocks, (0, 1), (0, 1), (0, 0)),
        K,
        targets,
        taper,
        partial,
        (north, south),
        panel,
        target_off=-1,
        emit=emit,
        edges=edges,
    )
    north2, south2 = lat_halo(first_row, last_row)
    row_fields = (1, 2) if lat_blocks == 2 else None
    partial = rows_call(
        own_plan(lat_blocks, 0, row_fields, (1, 0)),
        0,
        targets,
        taper,
        None,
        (wider, first_row, last_row),
        panel,
    )
    second_product = rows_call(
        halo_plan(lat_blocks, (0, 1), (2, 3), (1, 0)),
        0,
        targets,
        taper,
        partial,
        (north, south, north2, south2),
        panel,
    )
    return (first_product, second_product)


def solution(mesh):
    placed = (
        P("lat", "lon", None, None),
        P("lat", "lon", None, None),
        P("lat", "lon", None),
        P(None, "lat", "lon", None),
    )
    return jax.shard_map(
        local,
        mesh=mesh,
        in_specs=placed,
        out_specs=(P("lat", "lon", None, None), P("lat", "lon", None, None)),
        check_vma=False,
    )
```

```python
import functools

import numpy as np

import jax
import jax.numpy as jnp
from jax import lax
from jax.experimental import pallas as pl
from jax.experimental.pallas import tpu as pltpu
from jax.sharding import PartitionSpec as P

K = 80
COLS = 128
STRIDE = 16
RADIUS = 4
CODES = 9


def taper_by_code():
    codes = np.arange(CODES)
    shift_rows = ((codes // 3 - 1) * (COLS // STRIDE))[:, None, None]
    shift_cols = ((codes % 3 - 1) * STRIDE)[:, None, None]
    position = np.arange(COLS)
    row_within = position // STRIDE
    col_within = position % STRIDE
    delta_rows = shift_rows + (row_within[None, :] - row_within[:, None])
    delta_cols = shift_cols + (col_within[None, :] - col_within[:, None])
    squared = (delta_rows * delta_rows + delta_cols * delta_cols).astype(np.float32)
    f = np.float32
    scaled = np.sqrt(squared + f(0.25)) / f(RADIUS)
    inside = (
        ((f(-0.25) * scaled + f(0.5)) * scaled + f(0.625)) * scaled - f(5.0 / 3.0)
    ) * scaled * scaled + f(1.0)
    outside = (
        ((((scaled / f(12.0) - f(0.5)) * scaled + f(0.625)) * scaled + f(5.0 / 3.0)) * scaled - f(5.0)) * scaled
        + f(4.0)
        - f(2.0) / (f(3.0) * scaled)
    )
    table = np.where(scaled <= 1.0, inside, np.where(scaled <= 2.0, outside, f(0.0))).astype(np.float32)
    return jnp.asarray(table / f(K - 1))


def lon_halo(cells, depth):
    nlon = lax.axis_size("lon")
    west = lax.ppermute(cells[:, -depth:], "lon", [(i, (i + 1) % nlon) for i in range(nlon)])
    east = lax.ppermute(cells[:, :depth], "lon", [((i + 1) % nlon, i) for i in range(nlon)])
    return jnp.concatenate([west, cells, east], axis=1), west, east


def lat_halo(first_row, last_row):
    nlat = lax.axis_size("lat")
    north = lax.ppermute(last_row, "lat", [(i, i + 1) for i in range(nlat - 1)])
    south = lax.ppermute(first_row, "lat", [(i + 1, i) for i in range(nlat - 1)])
    return north, south


def rows_kernel(plan, field_at, with_partial, target_off, emit, targets_ref, edges_ref, taper_ref, *rest):
    outs = rest[-(1 + len(emit)) :] if emit else rest[-1:]
    rest = rest[: len(rest) - len(outs)]
    out_ref = outs[0]
    partial_ref = rest[0] if with_partial else None
    sources = rest[1:] if with_partial else rest
    columns, rank = out_ref.shape[2:]
    lat_blocks = out_ref.shape[0]
    lon_blocks = partial_ref.shape[1] if emit else out_ref.shape[1]
    for p in range(lat_blocks):

        def one_block(q, carry, p=p, uses=plan[p], side=None):
            if side is None:
                target = targets_ref[p, q + target_off]
            else:
                target = edges_ref[p, side]
            if with_partial:
                total = partial_ref[p, q]
            else:
                total = jnp.zeros((columns, rank), jnp.float32)
            for dr, members_at, members_row, field_from, row, members_off, field_off, trim in uses:
                members_ref, field_ref = sources[members_at], sources[field_from]
                for dc in range(3):
                    gram = jnp.dot(
                        target,
                        members_ref[members_row, q + dc + members_off, :K, :],
                        preferred_element_type=jnp.float32,
                    )
                    tile = gram * taper_ref[dr * 3 + dc]
                    tile_high = tile.astype(jnp.bfloat16)
                    tile_low = (tile - tile_high.astype(jnp.float32)).astype(jnp.bfloat16)
                    partner = field_ref.at[row, q + dc + field_off]
                    if trim:
                        kept = columns - STRIDE
                        pad = jnp.zeros((STRIDE, rank), jnp.bfloat16)
                        field_high = partner[field_at : field_at + kept, :]
                        field_low = partner[field_at + kept : field_at + 2 * kept, :]
                        if trim == 1:
                            field_high = jnp.concatenate([pad, field_high], axis=0)
                            field_low = jnp.concatenate([pad, field_low], axis=0)
                        else:
                            field_high = jnp.concatenate([field_high, pad], axis=0)
                            field_low = jnp.concatenate([field_low, pad], axis=0)
                    else:
                        field_high = partner[field_at : field_at + columns, :]
                        field_low = partner[field_at + columns : field_at + 2 * columns, :]
                    total = total + jnp.dot(tile_high, field_high, preferred_element_type=jnp.float32)
                    total = total + jnp.dot(tile_high, field_low, preferred_element_type=jnp.float32)
                    total = total + jnp.dot(tile_low, field_high, preferred_element_type=jnp.float32)
            if emit:
                inner = out_ref.shape[1]
                shift = (lon_blocks - inner) // 2

                @pl.when((q >= shift) & (q < shift + inner))
                def _():
                    out_ref[p, jnp.clip(q - shift, 0, inner - 1)] = total

                high = total.astype(jnp.bfloat16)
                low = (total - high.astype(jnp.float32)).astype(jnp.bfloat16)
                row_ref = outs[1 + emit[p]]
                row_ref[0, q, :columns, :] = high
                row_ref[0, q, columns:, :] = low
            else:
                out_ref[p, q] = total
            return carry

        if edges_ref is None:
            lax.fori_loop(0, lon_blocks, one_block, 0)
        else:
            one_block(0, 0, side=0)
            lax.fori_loop(1, lon_blocks - 1, one_block, 0)
            one_block(lon_blocks - 1, 0, side=1)


def kernel_with_edges(*args):
    return rows_kernel(*args)


def kernel_without_edges(plan, field_at, with_partial, target_off, emit, targets_ref, *rest):
    return rows_kernel(plan, field_at, with_partial, target_off, emit, targets_ref, None, *rest)


def rows_call(plan, field_at, targets, taper, partial, sources, out_like, target_off=0, emit=(), edges=None):
    lat_blocks, lon_blocks, columns, rank = (partial if emit else out_like).shape
    codes = sum(3 * len(uses) for uses in plan)
    flops = lon_blocks * codes * 2 * columns * (K * columns + 3 * columns * rank)
    operands = [targets] + ([edges] if edges is not None else []) + [taper]
    operands += ([partial] if partial is not None else []) + list(sources)
    shapes = [jax.ShapeDtypeStruct(out_like.shape, jnp.float32)]
    if emit:
        shapes += [jax.ShapeDtypeStruct((1, lon_blocks, 2 * columns, rank), jnp.bfloat16)] * len(emit)
    moved = sum(x.size * x.dtype.itemsize for x in operands + shapes)
    vmem = pl.BlockSpec(memory_space=pltpu.VMEM)
    result = pl.pallas_call(
        functools.partial(
            kernel_with_edges if edges is not None else kernel_without_edges,
            plan,
            field_at,
            partial is not None,
            target_off,
            emit,
        ),
        out_shape=tuple(shapes) if emit else shapes[0],
        in_specs=[vmem] * len(operands),
        out_specs=tuple([vmem] * len(shapes)) if emit else vmem,
        cost_estimate=pl.CostEstimate(flops=flops, bytes_accessed=moved, transcendentals=0),
    )(*operands)
    return result


def split_high_low(field):
    rounded = lax.reduce_precision(field, exponent_bits=8, mantissa_bits=7)
    return rounded.astype(jnp.bfloat16), (field - rounded).astype(jnp.bfloat16)


def own_plan(lat_blocks, members, fields, offsets):
    return tuple(
        tuple(
            (dr, members, p + dr - 1, fields[p + dr - 1], p + dr - 1 if len(set(fields)) == 1 else 0)
            + offsets
            + (0,)
            for dr in range(3)
            if 0 <= p + dr - 1 < lat_blocks
        )
        for p in range(lat_blocks)
    )


def halo_plan(lat_blocks, members, field, offsets, trimmed=False):
    return tuple(
        tuple(
            (dr, members[p + dr > 0], 0, field[p + dr > 0], 0)
            + offsets
            + ((1 if p + dr == 0 else 2) if trimmed else 0,)
            for dr in range(3)
            if not 0 <= p + dr - 1 < lat_blocks
        )
        for p in range(lat_blocks)
    )


def local(anomalies, panel, pair_code, pair_offset):
    del pair_code, pair_offset
    lat_blocks, lon_blocks = anomalies.shape[:2]
    taper = taper_by_code()
    panel_high, panel_low = split_high_low(panel)
    wider, west, east = lon_halo(jnp.concatenate([anomalies, panel_high, panel_low], axis=2), 2)
    kept = COLS - STRIDE
    going_north = jnp.concatenate(
        [wider[:1, :, :K], wider[:1, :, K : K + kept], wider[:1, :, K + COLS : K + COLS + kept]], axis=2
    )
    going_south = jnp.concatenate(
        [wider[-1:, :, :K], wider[-1:, :, K + STRIDE : K + COLS], wider[-1:, :, K + COLS + STRIDE :]], axis=2
    )
    north, south = lat_halo(going_north, going_south)
    targets = jnp.swapaxes(anomalies, 2, 3)
    edges = jnp.swapaxes(jnp.concatenate([west[:, 1:, :K, :], east[:, :1, :K, :]], axis=1), 2, 3)
    like_wide = jax.ShapeDtypeStruct((lat_blocks, lon_blocks + 2) + panel.shape[2:], jnp.float32)
    own_fields = (0,) * lat_blocks
    partial = rows_call(
        own_plan(lat_blocks, 0, own_fields, (0, 0)),
        K,
        targets,
        taper,
        None,
        (wider,),
        like_wide,
        target_off=-1,
        edges=edges,
    )
    emit = tuple(0 if p == 0 else 1 for p in range(lat_blocks))
    first_product, first_row, last_row = rows_call(
        halo_plan(lat_blocks, (0, 1), (0, 1), (0, 0), trimmed=True),
        K,
        targets,
        taper,
        partial,
        (north, south),
        panel,
        target_off=-1,
        emit=emit,
        edges=edges,
    )
    north2, south2 = lat_halo(first_row, last_row)
    row_fields = (1, 2) if lat_blocks == 2 else None
    partial = rows_call(
        own_plan(lat_blocks, 0, row_fields, (1, 0)),
        0,
        targets,
        taper,
        None,
        (wider, first_row, last_row),
        panel,
    )
    second_product = rows_call(
        halo_plan(lat_blocks, (0, 1), (2, 3), (1, 0)),
        0,
        targets,
        taper,
        partial,
        (north, south, north2, south2),
        panel,
    )
    return (first_product, second_product)


def solution(mesh):
    placed = (
        P("lat", "lon", None, None),
        P("lat", "lon", None, None),
        P("lat", "lon", None),
        P(None, "lat", "lon", None),
    )
    return jax.shard_map(
        local,
        mesh=mesh,
        in_specs=placed,
        out_specs=(P("lat", "lon", None, None), P("lat", "lon", None, None)),
        check_vma=False,
    )
```

```python
import functools

import numpy as np

import jax
import jax.numpy as jnp
from jax import lax
from jax.experimental import pallas as pl
from jax.experimental.pallas import tpu as pltpu
from jax.sharding import PartitionSpec as P

K = 80
COLS = 128
STRIDE = 16
RADIUS = 4
CODES = 9


def taper_by_code():
    codes = np.arange(CODES)
    shift_rows = ((codes // 3 - 1) * (COLS // STRIDE))[:, None, None]
    shift_cols = ((codes % 3 - 1) * STRIDE)[:, None, None]
    position = np.arange(COLS)
    row_within = position // STRIDE
    col_within = position % STRIDE
    delta_rows = shift_rows + (row_within[None, :] - row_within[:, None])
    delta_cols = shift_cols + (col_within[None, :] - col_within[:, None])
    squared = (delta_rows * delta_rows + delta_cols * delta_cols).astype(np.float32)
    f = np.float32
    scaled = np.sqrt(squared + f(0.25)) / f(RADIUS)
    inside = (
        ((f(-0.25) * scaled + f(0.5)) * scaled + f(0.625)) * scaled - f(5.0 / 3.0)
    ) * scaled * scaled + f(1.0)
    outside = (
        ((((scaled / f(12.0) - f(0.5)) * scaled + f(0.625)) * scaled + f(5.0 / 3.0)) * scaled - f(5.0)) * scaled
        + f(4.0)
        - f(2.0) / (f(3.0) * scaled)
    )
    table = np.where(scaled <= 1.0, inside, np.where(scaled <= 2.0, outside, f(0.0))).astype(np.float32)
    return jnp.asarray(table / f(K - 1))


def lon_halo(cells, depth):
    nlon = lax.axis_size("lon")
    west = lax.ppermute(cells[:, -depth:], "lon", [(i, (i + 1) % nlon) for i in range(nlon)])
    east = lax.ppermute(cells[:, :depth], "lon", [((i + 1) % nlon, i) for i in range(nlon)])
    return jnp.concatenate([west, cells, east], axis=1), west, east


def lat_halo(first_row, last_row):
    nlat = lax.axis_size("lat")
    north = lax.ppermute(last_row, "lat", [(i, i + 1) for i in range(nlat - 1)])
    south = lax.ppermute(first_row, "lat", [(i + 1, i) for i in range(nlat - 1)])
    return north, south


def rows_kernel(plan, field_at, with_partial, target_off, emit, targets_ref, edges_ref, taper_ref, *rest):
    outs = rest[-(1 + len(emit)) :] if emit else rest[-1:]
    rest = rest[: len(rest) - len(outs)]
    out_ref = outs[0]
    partial_ref = rest[0] if with_partial else None
    sources = rest[1:] if with_partial else rest
    columns, rank = out_ref.shape[2:]
    lat_blocks = out_ref.shape[0]
    lon_blocks = partial_ref.shape[1] if emit else out_ref.shape[1]
    for p in range(lat_blocks):

        def one_block(q, carry, p=p, uses=plan[p], side=None):
            if side is None:
                target = targets_ref[p, q + target_off]
            else:
                target = edges_ref[p, side]
            if with_partial:
                total = partial_ref[p, q]
            else:
                total = jnp.zeros((columns, rank), jnp.float32)
            for dr, members_at, members_row, field_from, row, members_off, field_off, trim in uses:
                members_ref, field_ref = sources[members_at], sources[field_from]
                for dc in range(3):
                    gram = jnp.dot(
                        target,
                        members_ref[members_row, q + dc + members_off, :K, :],
                        preferred_element_type=jnp.float32,
                    )
                    tile = gram * taper_ref[dr * 3 + dc]
                    tile_high = tile.astype(jnp.bfloat16)
                    tile_low = (tile - tile_high.astype(jnp.float32)).astype(jnp.bfloat16)
                    partner = field_ref.at[row, q + dc + field_off]
                    if trim:
                        kept = columns - STRIDE
                        pad = jnp.zeros((STRIDE, rank), jnp.bfloat16)
                        field_high = partner[field_at : field_at + kept, :]
                        field_low = partner[field_at + kept : field_at + 2 * kept, :]
                        if trim == 1:
                            field_high = jnp.concatenate([pad, field_high], axis=0)
                            field_low = jnp.concatenate([pad, field_low], axis=0)
                        else:
                            field_high = jnp.concatenate([field_high, pad], axis=0)
                            field_low = jnp.concatenate([field_low, pad], axis=0)
                    else:
                        field_high = partner[field_at : field_at + columns, :]
                        field_low = partner[field_at + columns : field_at + 2 * columns, :]
                    total = total + jnp.dot(tile_high, field_high, preferred_element_type=jnp.float32)
                    total = total + jnp.dot(tile_high, field_low, preferred_element_type=jnp.float32)
                    total = total + jnp.dot(tile_low, field_high, preferred_element_type=jnp.float32)
            if emit:
                inner = out_ref.shape[1]
                shift = (lon_blocks - inner) // 2

                @pl.when((q >= shift) & (q < shift + inner))
                def _():
                    out_ref[p, jnp.clip(q - shift, 0, inner - 1)] = total

                high = total.astype(jnp.bfloat16)
                low = (total - high.astype(jnp.float32)).astype(jnp.bfloat16)
                row_ref = outs[1 + emit[p]]
                row_ref[0, q, :columns, :] = high
                row_ref[0, q, columns:, :] = low
            else:
                out_ref[p, q] = total
            return carry

        if edges_ref is None:
            lax.fori_loop(0, lon_blocks, one_block, 0)
        else:
            one_block(0, 0, side=0)
            lax.fori_loop(1, lon_blocks - 1, one_block, 0)
            one_block(lon_blocks - 1, 0, side=1)


def kernel_with_edges(*args):
    return rows_kernel(*args)


def kernel_without_edges(plan, field_at, with_partial, target_off, emit, targets_ref, *rest):
    return rows_kernel(plan, field_at, with_partial, target_off, emit, targets_ref, None, *rest)


def rows_call(plan, field_at, targets, taper, partial, sources, out_like, target_off=0, emit=(), edges=None):
    lat_blocks, lon_blocks, columns, rank = (partial if emit else out_like).shape
    codes = sum(3 * len(uses) for uses in plan)
    flops = lon_blocks * codes * 2 * columns * (K * columns + 3 * columns * rank)
    operands = [targets] + ([edges] if edges is not None else []) + [taper]
    operands += ([partial] if partial is not None else []) + list(sources)
    shapes = [jax.ShapeDtypeStruct(out_like.shape, jnp.float32)]
    if emit:
        shapes += [jax.ShapeDtypeStruct((1, lon_blocks, 2 * columns, rank), jnp.bfloat16)] * len(emit)
    moved = sum(x.size * x.dtype.itemsize for x in operands + shapes)
    vmem = pl.BlockSpec(memory_space=pltpu.VMEM)
    result = pl.pallas_call(
        functools.partial(
            kernel_with_edges if edges is not None else kernel_without_edges,
            plan,
            field_at,
            partial is not None,
            target_off,
            emit,
        ),
        out_shape=tuple(shapes) if emit else shapes[0],
        in_specs=[vmem] * len(operands),
        out_specs=tuple([vmem] * len(shapes)) if emit else vmem,
        cost_estimate=pl.CostEstimate(flops=flops, bytes_accessed=moved, transcendentals=0),
    )(*operands)
    return result


def split_high_low(field):
    rounded = lax.reduce_precision(field, exponent_bits=8, mantissa_bits=7)
    return rounded.astype(jnp.bfloat16), (field - rounded).astype(jnp.bfloat16)


def own_plan(lat_blocks, members, fields, offsets):
    return tuple(
        tuple(
            (dr, members, p + dr - 1, fields[p + dr - 1], p + dr - 1 if len(set(fields)) == 1 else 0)
            + offsets
            + (0,)
            for dr in range(3)
            if 0 <= p + dr - 1 < lat_blocks
        )
        for p in range(lat_blocks)
    )


def halo_plan(lat_blocks, members, field, offsets, trimmed=False):
    return tuple(
        tuple(
            (dr, members[p + dr > 0], 0, field[p + dr > 0], 0)
            + offsets
            + ((1 if p + dr == 0 else 2) if trimmed else 0,)
            for dr in range(3)
            if not 0 <= p + dr - 1 < lat_blocks
        )
        for p in range(lat_blocks)
    )


def local(anomalies, panel, pair_code, pair_offset):
    del pair_code, pair_offset
    lat_blocks, lon_blocks = anomalies.shape[:2]
    taper = taper_by_code()
    panel_high, panel_low = split_high_low(panel)
    wider, west, east = lon_halo(jnp.concatenate([anomalies, panel_high, panel_low], axis=2), 2)
    kept = COLS - STRIDE

    def for_south_halo(rows):
        return jnp.concatenate(
            [rows[:, :, :K], rows[:, :, K : K + kept], rows[:, :, K + COLS : K + COLS + kept]], axis=2
        )

    def for_north_halo(rows):
        return jnp.concatenate(
            [rows[:, :, :K], rows[:, :, K + STRIDE : K + COLS], rows[:, :, K + COLS + STRIDE :]], axis=2
        )

    message = jnp.concatenate([anomalies, panel_high, panel_low], axis=2)
    north_own, south_own = lat_halo(for_south_halo(message[:1]), for_north_halo(message[-1:]))
    corners = jnp.concatenate([west, east], axis=1)
    north_corners, south_corners = lat_halo(for_south_halo(corners[:1]), for_north_halo(corners[-1:]))
    north = jnp.concatenate([north_corners[:, :2], north_own, north_corners[:, 2:]], axis=1)
    south = jnp.concatenate([south_corners[:, :2], south_own, south_corners[:, 2:]], axis=1)
    targets = jnp.swapaxes(anomalies, 2, 3)
    edges = jnp.swapaxes(jnp.concatenate([west[:, 1:, :K, :], east[:, :1, :K, :]], axis=1), 2, 3)
    like_wide = jax.ShapeDtypeStruct((lat_blocks, lon_blocks + 2) + panel.shape[2:], jnp.float32)
    own_fields = (0,) * lat_blocks
    partial = rows_call(
        own_plan(lat_blocks, 0, own_fields, (0, 0)),
        K,
        targets,
        taper,
        None,
        (wider,),
        like_wide,
        target_off=-1,
        edges=edges,
    )
    emit = tuple(0 if p == 0 else 1 for p in range(lat_blocks))
    first_product, first_row, last_row = rows_call(
        halo_plan(lat_blocks, (0, 1), (0, 1), (0, 0), trimmed=True),
        K,
        targets,
        taper,
        partial,
        (north, south),
        panel,
        target_off=-1,
        emit=emit,
        edges=edges,
    )
    north2, south2 = lat_halo(first_row, last_row)
    row_fields = (1, 2) if lat_blocks == 2 else None
    partial = rows_call(
        own_plan(lat_blocks, 0, row_fields, (1, 0)),
        0,
        targets,
        taper,
        None,
        (wider, first_row, last_row),
        panel,
    )
    second_product = rows_call(
        halo_plan(lat_blocks, (0, 1), (2, 3), (1, 0)),
        0,
        targets,
        taper,
        partial,
        (north, south, north2, south2),
        panel,
    )
    return (first_product, second_product)


def solution(mesh):
    placed = (
        P("lat", "lon", None, None),
        P("lat", "lon", None, None),
        P("lat", "lon", None),
        P(None, "lat", "lon", None),
    )
    return jax.shard_map(
        local,
        mesh=mesh,
        in_specs=placed,
        out_specs=(P("lat", "lon", None, None), P("lat", "lon", None, None)),
        check_vma=False,
    )
```

```python
import functools

import numpy as np

import jax
import jax.numpy as jnp
from jax import lax
from jax.experimental import pallas as pl
from jax.experimental.pallas import tpu as pltpu
from jax.sharding import PartitionSpec as P

K = 80
COLS = 128
STRIDE = 16
RADIUS = 4
CODES = 9


def taper_by_code():
    codes = np.arange(CODES)
    shift_rows = ((codes // 3 - 1) * (COLS // STRIDE))[:, None, None]
    shift_cols = ((codes % 3 - 1) * STRIDE)[:, None, None]
    position = np.arange(COLS)
    row_within = position // STRIDE
    col_within = position % STRIDE
    delta_rows = shift_rows + (row_within[None, :] - row_within[:, None])
    delta_cols = shift_cols + (col_within[None, :] - col_within[:, None])
    squared = (delta_rows * delta_rows + delta_cols * delta_cols).astype(np.float32)
    f = np.float32
    scaled = np.sqrt(squared + f(0.25)) / f(RADIUS)
    inside = (
        ((f(-0.25) * scaled + f(0.5)) * scaled + f(0.625)) * scaled - f(5.0 / 3.0)
    ) * scaled * scaled + f(1.0)
    outside = (
        ((((scaled / f(12.0) - f(0.5)) * scaled + f(0.625)) * scaled + f(5.0 / 3.0)) * scaled - f(5.0)) * scaled
        + f(4.0)
        - f(2.0) / (f(3.0) * scaled)
    )
    table = np.where(scaled <= 1.0, inside, np.where(scaled <= 2.0, outside, f(0.0))).astype(np.float32)
    return jnp.asarray(table / f(K - 1))


def lon_halo(cells, depth):
    nlon = lax.axis_size("lon")
    west = lax.ppermute(cells[:, -depth:], "lon", [(i, (i + 1) % nlon) for i in range(nlon)])
    east = lax.ppermute(cells[:, :depth], "lon", [((i + 1) % nlon, i) for i in range(nlon)])
    return jnp.concatenate([west, cells, east], axis=1), west, east


def lat_halo(first_row, last_row):
    nlat = lax.axis_size("lat")
    north = lax.ppermute(last_row, "lat", [(i, i + 1) for i in range(nlat - 1)])
    south = lax.ppermute(first_row, "lat", [(i + 1, i) for i in range(nlat - 1)])
    return north, south


def rows_kernel(plan, field_at, with_partial, target_off, emit, targets_ref, edges_ref, taper_ref, *rest):
    outs = rest[-(1 + len(emit)) :] if emit else rest[-1:]
    rest = rest[: len(rest) - len(outs)]
    out_ref = outs[0]
    partial_ref = rest[0] if with_partial else None
    sources = rest[1:] if with_partial else rest
    columns, rank = out_ref.shape[2:]
    lat_blocks = out_ref.shape[0]
    lon_blocks = partial_ref.shape[1] if emit else out_ref.shape[1]
    for p in range(lat_blocks):

        def one_block(q, carry, p=p, uses=plan[p], side=None):
            if side is None:
                target = targets_ref[p, q + target_off]
            else:
                target = edges_ref[p, side]
            if with_partial:
                total = partial_ref[p, q]
            else:
                total = jnp.zeros((columns, rank), jnp.float32)
            for dr, members_at, members_row, field_from, row, members_off, field_off, trim in uses:
                members_ref, field_ref = sources[members_at], sources[field_from]
                for dc in range(3):
                    gram = jnp.dot(
                        target,
                        members_ref[members_row, q + dc + members_off, :K, :],
                        preferred_element_type=jnp.float32,
                    )
                    tile = gram * taper_ref[dr * 3 + dc]
                    tile_high = tile.astype(jnp.bfloat16)
                    tile_low = (tile - tile_high.astype(jnp.float32)).astype(jnp.bfloat16)
                    partner = field_ref.at[row, q + dc + field_off]
                    if trim:
                        kept = columns - STRIDE
                        pad = jnp.zeros((STRIDE, rank), jnp.bfloat16)
                        field_high = partner[field_at : field_at + kept, :]
                        field_low = partner[field_at + kept : field_at + 2 * kept, :]
                        if trim == 1:
                            field_high = jnp.concatenate([pad, field_high], axis=0)
                            field_low = jnp.concatenate([pad, field_low], axis=0)
                        else:
                            field_high = jnp.concatenate([field_high, pad], axis=0)
                            field_low = jnp.concatenate([field_low, pad], axis=0)
                    else:
                        field_high = partner[field_at : field_at + columns, :]
                        field_low = partner[field_at + columns : field_at + 2 * columns, :]
                    total = total + jnp.dot(tile_high, field_high, preferred_element_type=jnp.float32)
                    total = total + jnp.dot(tile_high, field_low, preferred_element_type=jnp.float32)
                    total = total + jnp.dot(tile_low, field_high, preferred_element_type=jnp.float32)
            if emit:
                inner = out_ref.shape[1]
                shift = (lon_blocks - inner) // 2

                @pl.when((q >= shift) & (q < shift + inner))
                def _():
                    out_ref[p, jnp.clip(q - shift, 0, inner - 1)] = total

                high = total.astype(jnp.bfloat16)
                low = (total - high.astype(jnp.float32)).astype(jnp.bfloat16)
                row_ref = outs[1 + emit[p]]
                row_ref[0, q, :columns, :] = high
                row_ref[0, q, columns:, :] = low
            else:
                out_ref[p, q] = total
            return carry

        if edges_ref is None:
            lax.fori_loop(0, lon_blocks, one_block, 0)
        else:
            one_block(0, 0, side=0)
            lax.fori_loop(1, lon_blocks - 1, one_block, 0)
            one_block(lon_blocks - 1, 0, side=1)


def kernel_with_edges(*args):
    return rows_kernel(*args)


def kernel_without_edges(plan, field_at, with_partial, target_off, emit, targets_ref, *rest):
    return rows_kernel(plan, field_at, with_partial, target_off, emit, targets_ref, None, *rest)


def rows_call(plan, field_at, targets, taper, partial, sources, out_like, target_off=0, emit=(), edges=None):
    lat_blocks, lon_blocks, columns, rank = (partial if emit else out_like).shape
    codes = sum(3 * len(uses) for uses in plan)
    flops = lon_blocks * codes * 2 * columns * (K * columns + 3 * columns * rank)
    operands = [targets] + ([edges] if edges is not None else []) + [taper]
    operands += ([partial] if partial is not None else []) + list(sources)
    shapes = [jax.ShapeDtypeStruct(out_like.shape, jnp.float32)]
    if emit:
        shapes += [jax.ShapeDtypeStruct((1, lon_blocks, 2 * columns, rank), jnp.bfloat16)] * len(emit)
    moved = sum(x.size * x.dtype.itemsize for x in operands + shapes)
    vmem = pl.BlockSpec(memory_space=pltpu.VMEM)
    result = pl.pallas_call(
        functools.partial(
            kernel_with_edges if edges is not None else kernel_without_edges,
            plan,
            field_at,
            partial is not None,
            target_off,
            emit,
        ),
        out_shape=tuple(shapes) if emit else shapes[0],
        in_specs=[vmem] * len(operands),
        out_specs=tuple([vmem] * len(shapes)) if emit else vmem,
        cost_estimate=pl.CostEstimate(flops=flops, bytes_accessed=moved, transcendentals=0),
    )(*operands)
    return result


def split_high_low(field):
    rounded = lax.reduce_precision(field, exponent_bits=8, mantissa_bits=7)
    return rounded.astype(jnp.bfloat16), (field - rounded).astype(jnp.bfloat16)


def own_plan(lat_blocks, members, fields, offsets):
    return tuple(
        tuple(
            (dr, members, p + dr - 1, fields[p + dr - 1], p + dr - 1 if len(set(fields)) == 1 else 0)
            + offsets
            + (0,)
            for dr in range(3)
            if 0 <= p + dr - 1 < lat_blocks
        )
        for p in range(lat_blocks)
    )


def halo_plan(lat_blocks, members, field, offsets, trimmed=False):
    return tuple(
        tuple(
            (dr, members[p + dr > 0], 0, field[p + dr > 0], 0)
            + offsets
            + ((1 if p + dr == 0 else 2) if trimmed else 0,)
            for dr in range(3)
            if not 0 <= p + dr - 1 < lat_blocks
        )
        for p in range(lat_blocks)
    )


def local(anomalies, panel, pair_code, pair_offset):
    del pair_code, pair_offset
    lat_blocks, lon_blocks = anomalies.shape[:2]
    taper = taper_by_code()
    panel_high, panel_low = split_high_low(panel)
    wider, west, east = lon_halo(jnp.concatenate([anomalies, panel_high, panel_low], axis=2), 2)
    kept = COLS - STRIDE
    going_north = jnp.concatenate(
        [wider[:1, :, :K], wider[:1, :, K : K + kept], wider[:1, :, K + COLS : K + COLS + kept]], axis=2
    )
    going_south = jnp.concatenate(
        [wider[-1:, :, :K], wider[-1:, :, K + STRIDE : K + COLS], wider[-1:, :, K + COLS + STRIDE :]], axis=2
    )
    north, south = lat_halo(going_north, going_south)
    targets = jnp.swapaxes(anomalies, 2, 3)
    edges = jnp.swapaxes(jnp.concatenate([west[:, 1:, :K, :], east[:, :1, :K, :]], axis=1), 2, 3)
    like_wide = jax.ShapeDtypeStruct((lat_blocks, lon_blocks + 2) + panel.shape[2:], jnp.float32)
    own_fields = (0,) * lat_blocks
    partial = rows_call(
        own_plan(lat_blocks, 0, own_fields, (0, 0)),
        K,
        targets,
        taper,
        None,
        (wider,),
        like_wide,
        target_off=-1,
        edges=edges,
    )
    emit = tuple(0 if p == 0 else 1 for p in range(lat_blocks))
    first_product, first_row, last_row = rows_call(
        halo_plan(lat_blocks, (0, 1), (0, 1), (0, 0), trimmed=True),
        K,
        targets,
        taper,
        partial,
        (north, south),
        panel,
        target_off=-1,
        emit=emit,
        edges=edges,
    )
    north2, south2 = lat_halo(first_row, last_row)
    row_fields = (1, 2) if lat_blocks == 2 else None
    members = wider[:, 1 : lon_blocks + 3, :K]
    members_north = north[:, 1 : lon_blocks + 3, :K]
    members_south = south[:, 1 : lon_blocks + 3, :K]
    partial = rows_call(
        own_plan(lat_blocks, 0, row_fields, (0, 0)),
        0,
        targets,
        taper,
        None,
        (members, first_row, last_row),
        panel,
    )
    second_product = rows_call(
        halo_plan(lat_blocks, (0, 1), (2, 3), (0, 0)),
        0,
        targets,
        taper,
        partial,
        (members_north, members_south, north2, south2),
        panel,
    )
    return (first_product, second_product)


def solution(mesh):
    placed = (
        P("lat", "lon", None, None),
        P("lat", "lon", None, None),
        P("lat", "lon", None),
        P(None, "lat", "lon", None),
    )
    return jax.shard_map(
        local,
        mesh=mesh,
        in_specs=placed,
        out_specs=(P("lat", "lon", None, None), P("lat", "lon", None, None)),
        check_vma=False,
    )
```

```python
import functools

import numpy as np

import jax
import jax.numpy as jnp
from jax import lax
from jax.experimental import pallas as pl
from jax.experimental.pallas import tpu as pltpu
from jax.sharding import PartitionSpec as P

K = 80
COLS = 128
STRIDE = 16
RADIUS = 4
CODES = 9


def taper_by_code():
    codes = np.arange(CODES)
    shift_rows = ((codes // 3 - 1) * (COLS // STRIDE))[:, None, None]
    shift_cols = ((codes % 3 - 1) * STRIDE)[:, None, None]
    position = np.arange(COLS)
    row_within = position // STRIDE
    col_within = position % STRIDE
    delta_rows = shift_rows + (row_within[None, :] - row_within[:, None])
    delta_cols = shift_cols + (col_within[None, :] - col_within[:, None])
    squared = (delta_rows * delta_rows + delta_cols * delta_cols).astype(np.float32)
    f = np.float32
    scaled = np.sqrt(squared + f(0.25)) / f(RADIUS)
    inside = (
        ((f(-0.25) * scaled + f(0.5)) * scaled + f(0.625)) * scaled - f(5.0 / 3.0)
    ) * scaled * scaled + f(1.0)
    outside = (
        ((((scaled / f(12.0) - f(0.5)) * scaled + f(0.625)) * scaled + f(5.0 / 3.0)) * scaled - f(5.0)) * scaled
        + f(4.0)
        - f(2.0) / (f(3.0) * scaled)
    )
    table = np.where(scaled <= 1.0, inside, np.where(scaled <= 2.0, outside, f(0.0))).astype(np.float32)
    return jnp.asarray(table / f(K - 1))


def lon_halo(cells, depth):
    nlon = lax.axis_size("lon")
    west = lax.ppermute(cells[:, -depth:], "lon", [(i, (i + 1) % nlon) for i in range(nlon)])
    east = lax.ppermute(cells[:, :depth], "lon", [((i + 1) % nlon, i) for i in range(nlon)])
    return jnp.concatenate([west, cells, east], axis=1), west, east


def lat_halo(first_row, last_row):
    nlat = lax.axis_size("lat")
    north = lax.ppermute(last_row, "lat", [(i, i + 1) for i in range(nlat - 1)])
    south = lax.ppermute(first_row, "lat", [(i + 1, i) for i in range(nlat - 1)])
    return north, south


def rows_kernel(plan, field_at, with_partial, target_off, emit, copies, targets_ref, edges_ref, taper_ref, *rest):
    count = 1 + len(emit) + len(copies)
    outs = rest[-count:]
    rest = rest[: len(rest) - count]
    out_ref = outs[0]
    partial_ref = rest[0] if with_partial else None
    sources = rest[1:] if with_partial else rest
    for (source, first, end), copy_ref in zip(copies, outs[1 + len(emit) :]):
        copy_ref[...] = sources[source][:, first:end, :K, :]
    columns, rank = out_ref.shape[2:]
    lat_blocks = out_ref.shape[0]
    lon_blocks = partial_ref.shape[1] if emit else out_ref.shape[1]
    for p in range(lat_blocks):

        def one_block(q, carry, p=p, uses=plan[p], side=None):
            if side is None:
                target = targets_ref[p, q + target_off]
            else:
                target = edges_ref[p, side]
            if with_partial:
                total = partial_ref[p, q]
            else:
                total = jnp.zeros((columns, rank), jnp.float32)
            for dr, members_at, members_row, field_from, row, members_off, field_off, trim in uses:
                members_ref, field_ref = sources[members_at], sources[field_from]
                for dc in range(3):
                    gram = jnp.dot(
                        target,
                        members_ref[members_row, q + dc + members_off, :K, :],
                        preferred_element_type=jnp.float32,
                    )
                    tile = gram * taper_ref[dr * 3 + dc]
                    tile_high = tile.astype(jnp.bfloat16)
                    tile_low = (tile - tile_high.astype(jnp.float32)).astype(jnp.bfloat16)
                    partner = field_ref.at[row, q + dc + field_off]
                    if trim:
                        kept = columns - STRIDE
                        pad = jnp.zeros((STRIDE, rank), jnp.bfloat16)
                        field_high = partner[field_at : field_at + kept, :]
                        field_low = partner[field_at + kept : field_at + 2 * kept, :]
                        if trim == 1:
                            field_high = jnp.concatenate([pad, field_high], axis=0)
                            field_low = jnp.concatenate([pad, field_low], axis=0)
                        else:
                            field_high = jnp.concatenate([field_high, pad], axis=0)
                            field_low = jnp.concatenate([field_low, pad], axis=0)
                    else:
                        field_high = partner[field_at : field_at + columns, :]
                        field_low = partner[field_at + columns : field_at + 2 * columns, :]
                    total = total + jnp.dot(tile_high, field_high, preferred_element_type=jnp.float32)
                    total = total + jnp.dot(tile_high, field_low, preferred_element_type=jnp.float32)
                    total = total + jnp.dot(tile_low, field_high, preferred_element_type=jnp.float32)
            if emit:
                inner = out_ref.shape[1]
                shift = (lon_blocks - inner) // 2

                @pl.when((q >= shift) & (q < shift + inner))
                def _():
                    out_ref[p, jnp.clip(q - shift, 0, inner - 1)] = total

                high = total.astype(jnp.bfloat16)
                low = (total - high.astype(jnp.float32)).astype(jnp.bfloat16)
                row_ref = outs[1 + emit[p]]
                row_ref[0, q, :columns, :] = high
                row_ref[0, q, columns:, :] = low
            else:
                out_ref[p, q] = total
            return carry

        if edges_ref is None:
            lax.fori_loop(0, lon_blocks, one_block, 0)
        else:
            one_block(0, 0, side=0)
            lax.fori_loop(1, lon_blocks - 1, one_block, 0)
            one_block(lon_blocks - 1, 0, side=1)


def kernel_with_edges(*args):
    return rows_kernel(*args)


def kernel_without_edges(plan, field_at, with_partial, target_off, emit, copies, targets_ref, *rest):
    return rows_kernel(plan, field_at, with_partial, target_off, emit, copies, targets_ref, None, *rest)


def rows_call(
    plan, field_at, targets, taper, partial, sources, out_like, target_off=0, emit=(), edges=None, copies=()
):
    lat_blocks, lon_blocks, columns, rank = (partial if emit else out_like).shape
    codes = sum(3 * len(uses) for uses in plan)
    flops = lon_blocks * codes * 2 * columns * (K * columns + 3 * columns * rank)
    operands = [targets] + ([edges] if edges is not None else []) + [taper]
    operands += ([partial] if partial is not None else []) + list(sources)
    shapes = [jax.ShapeDtypeStruct(out_like.shape, jnp.float32)]
    if emit:
        shapes += [jax.ShapeDtypeStruct((1, lon_blocks, 2 * columns, rank), jnp.bfloat16)] * len(emit)
    for source, first, end in copies:
        held = sources[source]
        shapes.append(jax.ShapeDtypeStruct((held.shape[0], end - first, K, held.shape[3]), held.dtype))
    several = len(shapes) > 1
    moved = sum(x.size * x.dtype.itemsize for x in operands + shapes)
    vmem = pl.BlockSpec(memory_space=pltpu.VMEM)
    result = pl.pallas_call(
        functools.partial(
            kernel_with_edges if edges is not None else kernel_without_edges,
            plan,
            field_at,
            partial is not None,
            target_off,
            emit,
            copies,
        ),
        out_shape=tuple(shapes) if several else shapes[0],
        in_specs=[vmem] * len(operands),
        out_specs=tuple([vmem] * len(shapes)) if several else vmem,
        cost_estimate=pl.CostEstimate(flops=flops, bytes_accessed=moved, transcendentals=0),
    )(*operands)
    return result


def split_high_low(field):
    rounded = lax.reduce_precision(field, exponent_bits=8, mantissa_bits=7)
    return rounded.astype(jnp.bfloat16), (field - rounded).astype(jnp.bfloat16)


def own_plan(lat_blocks, members, fields, offsets):
    return tuple(
        tuple(
            (dr, members, p + dr - 1, fields[p + dr - 1], p + dr - 1 if len(set(fields)) == 1 else 0)
            + offsets
            + (0,)
            for dr in range(3)
            if 0 <= p + dr - 1 < lat_blocks
        )
        for p in range(lat_blocks)
    )


def halo_plan(lat_blocks, members, field, offsets, trimmed=False):
    return tuple(
        tuple(
            (dr, members[p + dr > 0], 0, field[p + dr > 0], 0)
            + offsets
            + ((1 if p + dr == 0 else 2) if trimmed else 0,)
            for dr in range(3)
            if not 0 <= p + dr - 1 < lat_blocks
        )
        for p in range(lat_blocks)
    )


def local(anomalies, panel, pair_code, pair_offset):
    del pair_code, pair_offset
    lat_blocks, lon_blocks = anomalies.shape[:2]
    taper = taper_by_code()
    panel_high, panel_low = split_high_low(panel)
    wider, west, east = lon_halo(jnp.concatenate([anomalies, panel_high, panel_low], axis=2), 2)
    kept = COLS - STRIDE
    going_north = jnp.concatenate(
        [wider[:1, :, :K], wider[:1, :, K : K + kept], wider[:1, :, K + COLS : K + COLS + kept]], axis=2
    )
    going_south = jnp.concatenate(
        [wider[-1:, :, :K], wider[-1:, :, K + STRIDE : K + COLS], wider[-1:, :, K + COLS + STRIDE :]], axis=2
    )
    north, south = lat_halo(going_north, going_south)
    targets = jnp.swapaxes(anomalies, 2, 3)
    edges = jnp.swapaxes(jnp.concatenate([west[:, 1:, :K, :], east[:, :1, :K, :]], axis=1), 2, 3)
    like_wide = jax.ShapeDtypeStruct((lat_blocks, lon_blocks + 2) + panel.shape[2:], jnp.float32)
    own_fields = (0,) * lat_blocks
    span = (1, lon_blocks + 3)
    partial, members = rows_call(
        own_plan(lat_blocks, 0, own_fields, (0, 0)),
        K,
        targets,
        taper,
        None,
        (wider,),
        like_wide,
        target_off=-1,
        edges=edges,
        copies=((0,) + span,),
    )
    emit = tuple(0 if p == 0 else 1 for p in range(lat_blocks))
    first_product, first_row, last_row, members_north, members_south = rows_call(
        halo_plan(lat_blocks, (0, 1), (0, 1), (0, 0), trimmed=True),
        K,
        targets,
        taper,
        partial,
        (north, south),
        panel,
        target_off=-1,
        emit=emit,
        edges=edges,
        copies=((0,) + span, (1,) + span),
    )
    north2, south2 = lat_halo(first_row, last_row)
    row_fields = (1, 2) if lat_blocks == 2 else None
    partial = rows_call(
        own_plan(lat_blocks, 0, row_fields, (0, 0)),
        0,
        targets,
        taper,
        None,
        (members, first_row, last_row),
        panel,
    )
    second_product = rows_call(
        halo_plan(lat_blocks, (0, 1), (2, 3), (0, 0)),
        0,
        targets,
        taper,
        partial,
        (members_north, members_south, north2, south2),
        panel,
    )
    return (first_product, second_product)


def solution(mesh):
    placed = (
        P("lat", "lon", None, None),
        P("lat", "lon", None, None),
        P("lat", "lon", None),
        P(None, "lat", "lon", None),
    )
    return jax.shard_map(
        local,
        mesh=mesh,
        in_specs=placed,
        out_specs=(P("lat", "lon", None, None), P("lat", "lon", None, None)),
        check_vma=False,
    )
```

```python
import functools

import numpy as np

import jax
import jax.numpy as jnp
from jax import lax
from jax.experimental import pallas as pl
from jax.experimental.pallas import tpu as pltpu
from jax.sharding import PartitionSpec as P

K = 80
COLS = 128
STRIDE = 16
RADIUS = 4
CODES = 9


def taper_by_code():
    codes = np.arange(CODES)
    shift_rows = ((codes // 3 - 1) * (COLS // STRIDE))[:, None, None]
    shift_cols = ((codes % 3 - 1) * STRIDE)[:, None, None]
    position = np.arange(COLS)
    row_within = position // STRIDE
    col_within = position % STRIDE
    delta_rows = shift_rows + (row_within[None, :] - row_within[:, None])
    delta_cols = shift_cols + (col_within[None, :] - col_within[:, None])
    squared = (delta_rows * delta_rows + delta_cols * delta_cols).astype(np.float32)
    f = np.float32
    scaled = np.sqrt(squared + f(0.25)) / f(RADIUS)
    inside = (
        ((f(-0.25) * scaled + f(0.5)) * scaled + f(0.625)) * scaled - f(5.0 / 3.0)
    ) * scaled * scaled + f(1.0)
    outside = (
        ((((scaled / f(12.0) - f(0.5)) * scaled + f(0.625)) * scaled + f(5.0 / 3.0)) * scaled - f(5.0)) * scaled
        + f(4.0)
        - f(2.0) / (f(3.0) * scaled)
    )
    table = np.where(scaled <= 1.0, inside, np.where(scaled <= 2.0, outside, f(0.0))).astype(np.float32)
    return jnp.asarray(table / f(K - 1))


def lon_halo(cells, depth):
    nlon = lax.axis_size("lon")
    west = lax.ppermute(cells[:, -depth:], "lon", [(i, (i + 1) % nlon) for i in range(nlon)])
    east = lax.ppermute(cells[:, :depth], "lon", [((i + 1) % nlon, i) for i in range(nlon)])
    return jnp.concatenate([west, cells, east], axis=1), west, east


def lat_halo(first_row, last_row):
    nlat = lax.axis_size("lat")
    north = lax.ppermute(last_row, "lat", [(i, i + 1) for i in range(nlat - 1)])
    south = lax.ppermute(first_row, "lat", [(i + 1, i) for i in range(nlat - 1)])
    return north, south


def rows_kernel(
    plan, field_at, with_partial, target_off, emit, copies, tiles, targets_ref, edges_ref, taper_ref, *rest
):
    count = 1 + len(emit) + len(copies) + (tiles == "save")
    outs = rest[-count:]
    rest = rest[: len(rest) - count]
    out_ref = outs[0]
    partial_ref = rest[0] if with_partial else None
    sources = rest[1:] if with_partial else rest
    tiles_ref = outs[-1] if tiles == "save" else (sources[-1] if tiles == "load" else None)
    for (source, first, end), copy_ref in zip(copies, outs[1 + len(emit) :]):
        copy_ref[...] = sources[source][:, first:end, :K, :]
    columns, rank = out_ref.shape[2:]
    lat_blocks = out_ref.shape[0]
    lon_blocks = partial_ref.shape[1] if emit else out_ref.shape[1]
    for p in range(lat_blocks):

        def one_block(q, carry, p=p, uses=plan[p], side=None, middle=False):
            if side is None:
                target = targets_ref[p, q + target_off]
            else:
                target = edges_ref[p, side]
            if with_partial:
                total = partial_ref[p, q]
            else:
                total = jnp.zeros((columns, rank), jnp.float32)
            for dr, members_at, members_row, field_from, row, members_off, field_off, trim in uses:
                members_ref, field_ref = sources[members_at], sources[field_from]
                for dc in range(3):
                    slot = 3 * uses.index((dr, members_at, members_row, field_from, row, members_off, field_off, trim)) + dc
                    if tiles == "load":
                        tile_high = tiles_ref[p, q, slot, :columns, :]
                        tile_low = tiles_ref[p, q, slot, columns:, :]
                    else:
                        gram = jnp.dot(
                            target,
                            members_ref[members_row, q + dc + members_off, :K, :],
                            preferred_element_type=jnp.float32,
                        )
                        tile = gram * taper_ref[dr * 3 + dc]
                        tile_high = tile.astype(jnp.bfloat16)
                        tile_low = (tile - tile_high.astype(jnp.float32)).astype(jnp.bfloat16)
                        if tiles == "save" and middle:
                            tiles_ref[p, q - 1, slot, :columns, :] = tile_high
                            tiles_ref[p, q - 1, slot, columns:, :] = tile_low
                    partner = field_ref.at[row, q + dc + field_off]
                    if trim:
                        kept = columns - STRIDE
                        pad = jnp.zeros((STRIDE, rank), jnp.bfloat16)
                        field_high = partner[field_at : field_at + kept, :]
                        field_low = partner[field_at + kept : field_at + 2 * kept, :]
                        if trim == 1:
                            field_high = jnp.concatenate([pad, field_high], axis=0)
                            field_low = jnp.concatenate([pad, field_low], axis=0)
                        else:
                            field_high = jnp.concatenate([field_high, pad], axis=0)
                            field_low = jnp.concatenate([field_low, pad], axis=0)
                    else:
                        field_high = partner[field_at : field_at + columns, :]
                        field_low = partner[field_at + columns : field_at + 2 * columns, :]
                    total = total + jnp.dot(tile_high, field_high, preferred_element_type=jnp.float32)
                    total = total + jnp.dot(tile_high, field_low, preferred_element_type=jnp.float32)
                    total = total + jnp.dot(tile_low, field_high, preferred_element_type=jnp.float32)
            if emit:
                inner = out_ref.shape[1]
                shift = (lon_blocks - inner) // 2

                @pl.when((q >= shift) & (q < shift + inner))
                def _():
                    out_ref[p, jnp.clip(q - shift, 0, inner - 1)] = total

                high = total.astype(jnp.bfloat16)
                low = (total - high.astype(jnp.float32)).astype(jnp.bfloat16)
                row_ref = outs[1 + emit[p]]
                row_ref[0, q, :columns, :] = high
                row_ref[0, q, columns:, :] = low
            else:
                out_ref[p, q] = total
            return carry

        if edges_ref is None:
            lax.fori_loop(0, lon_blocks, one_block, 0)
        else:
            one_block(0, 0, side=0)
            lax.fori_loop(1, lon_blocks - 1, functools.partial(one_block, middle=True), 0)
            one_block(lon_blocks - 1, 0, side=1)


def kernel_with_edges(*args):
    return rows_kernel(*args)


def kernel_without_edges(plan, field_at, with_partial, target_off, emit, copies, tiles, targets_ref, *rest):
    return rows_kernel(plan, field_at, with_partial, target_off, emit, copies, tiles, targets_ref, None, *rest)


def rows_call(
    plan,
    field_at,
    targets,
    taper,
    partial,
    sources,
    out_like,
    target_off=0,
    emit=(),
    edges=None,
    copies=(),
    tiles=None,
):
    lat_blocks, lon_blocks, columns, rank = (partial if emit else out_like).shape
    codes = sum(3 * len(uses) for uses in plan)
    flops = lon_blocks * codes * 2 * columns * (K * columns + 3 * columns * rank)
    operands = [targets] + ([edges] if edges is not None else []) + [taper]
    operands += ([partial] if partial is not None else []) + list(sources)
    shapes = [jax.ShapeDtypeStruct(out_like.shape, jnp.float32)]
    if emit:
        shapes += [jax.ShapeDtypeStruct((1, lon_blocks, 2 * columns, rank), jnp.bfloat16)] * len(emit)
    for source, first, end in copies:
        held = sources[source]
        shapes.append(jax.ShapeDtypeStruct((held.shape[0], end - first, K, held.shape[3]), held.dtype))
    if tiles == "save":
        slots = max(3 * len(uses) for uses in plan)
        inner = lon_blocks - 2
        shapes.append(jax.ShapeDtypeStruct((lat_blocks, inner, slots, 2 * columns, rank), jnp.bfloat16))
    several = len(shapes) > 1
    moved = sum(x.size * x.dtype.itemsize for x in operands + shapes)
    vmem = pl.BlockSpec(memory_space=pltpu.VMEM)
    result = pl.pallas_call(
        functools.partial(
            kernel_with_edges if edges is not None else kernel_without_edges,
            plan,
            field_at,
            partial is not None,
            target_off,
            emit,
            copies,
            tiles,
        ),
        out_shape=tuple(shapes) if several else shapes[0],
        in_specs=[vmem] * len(operands),
        out_specs=tuple([vmem] * len(shapes)) if several else vmem,
        cost_estimate=pl.CostEstimate(flops=flops, bytes_accessed=moved, transcendentals=0),
    )(*operands)
    return result


def split_high_low(field):
    rounded = lax.reduce_precision(field, exponent_bits=8, mantissa_bits=7)
    return rounded.astype(jnp.bfloat16), (field - rounded).astype(jnp.bfloat16)


def own_plan(lat_blocks, members, fields, offsets):
    return tuple(
        tuple(
            (dr, members, p + dr - 1, fields[p + dr - 1], p + dr - 1 if len(set(fields)) == 1 else 0)
            + offsets
            + (0,)
            for dr in range(3)
            if 0 <= p + dr - 1 < lat_blocks
        )
        for p in range(lat_blocks)
    )


def halo_plan(lat_blocks, members, field, offsets, trimmed=False):
    return tuple(
        tuple(
            (dr, members[p + dr > 0], 0, field[p + dr > 0], 0)
            + offsets
            + ((1 if p + dr == 0 else 2) if trimmed else 0,)
            for dr in range(3)
            if not 0 <= p + dr - 1 < lat_blocks
        )
        for p in range(lat_blocks)
    )


def local(anomalies, panel, pair_code, pair_offset):
    del pair_code, pair_offset
    lat_blocks, lon_blocks = anomalies.shape[:2]
    taper = taper_by_code()
    panel_high, panel_low = split_high_low(panel)
    wider, west, east = lon_halo(jnp.concatenate([anomalies, panel_high, panel_low], axis=2), 2)
    kept = COLS - STRIDE
    going_north = jnp.concatenate(
        [wider[:1, :, :K], wider[:1, :, K : K + kept], wider[:1, :, K + COLS : K + COLS + kept]], axis=2
    )
    going_south = jnp.concatenate(
        [wider[-1:, :, :K], wider[-1:, :, K + STRIDE : K + COLS], wider[-1:, :, K + COLS + STRIDE :]], axis=2
    )
    north, south = lat_halo(going_north, going_south)
    targets = jnp.swapaxes(anomalies, 2, 3)
    edges = jnp.swapaxes(jnp.concatenate([west[:, 1:, :K, :], east[:, :1, :K, :]], axis=1), 2, 3)
    like_wide = jax.ShapeDtypeStruct((lat_blocks, lon_blocks + 2) + panel.shape[2:], jnp.float32)
    own_fields = (0,) * lat_blocks
    span = (1, lon_blocks + 3)
    partial, members, own_tiles = rows_call(
        own_plan(lat_blocks, 0, own_fields, (0, 0)),
        K,
        targets,
        taper,
        None,
        (wider,),
        like_wide,
        target_off=-1,
        edges=edges,
        copies=((0,) + span,),
        tiles="save",
    )
    emit = tuple(0 if p == 0 else 1 for p in range(lat_blocks))
    first_product, first_row, last_row, members_north, members_south = rows_call(
        halo_plan(lat_blocks, (0, 1), (0, 1), (0, 0), trimmed=True),
        K,
        targets,
        taper,
        partial,
        (north, south),
        panel,
        target_off=-1,
        emit=emit,
        edges=edges,
        copies=((0,) + span, (1,) + span),
    )
    north2, south2 = lat_halo(first_row, last_row)
    row_fields = (1, 2) if lat_blocks == 2 else None
    partial = rows_call(
        own_plan(lat_blocks, 0, row_fields, (0, 0)),
        0,
        targets,
        taper,
        None,
        (members, first_row, last_row, own_tiles),
        panel,
        tiles="load",
    )
    second_product = rows_call(
        halo_plan(lat_blocks, (0, 1), (2, 3), (0, 0)),
        0,
        targets,
        taper,
        partial,
        (members_north, members_south, north2, south2),
        panel,
    )
    return (first_product, second_product)


def solution(mesh):
    placed = (
        P("lat", "lon", None, None),
        P("lat", "lon", None, None),
        P("lat", "lon", None),
        P(None, "lat", "lon", None),
    )
    return jax.shard_map(
        local,
        mesh=mesh,
        in_specs=placed,
        out_specs=(P("lat", "lon", None, None), P("lat", "lon", None, None)),
        check_vma=False,
    )
```

```python
import functools

import numpy as np

import jax
import jax.numpy as jnp
from jax import lax
from jax.experimental import pallas as pl
from jax.experimental.pallas import tpu as pltpu
from jax.sharding import PartitionSpec as P

K = 80
COLS = 128
STRIDE = 16
RADIUS = 4
CODES = 9


def taper_by_code():
    codes = np.arange(CODES)
    shift_rows = ((codes // 3 - 1) * (COLS // STRIDE))[:, None, None]
    shift_cols = ((codes % 3 - 1) * STRIDE)[:, None, None]
    position = np.arange(COLS)
    row_within = position // STRIDE
    col_within = position % STRIDE
    delta_rows = shift_rows + (row_within[None, :] - row_within[:, None])
    delta_cols = shift_cols + (col_within[None, :] - col_within[:, None])
    squared = (delta_rows * delta_rows + delta_cols * delta_cols).astype(np.float32)
    f = np.float32
    scaled = np.sqrt(squared + f(0.25)) / f(RADIUS)
    inside = (
        ((f(-0.25) * scaled + f(0.5)) * scaled + f(0.625)) * scaled - f(5.0 / 3.0)
    ) * scaled * scaled + f(1.0)
    outside = (
        ((((scaled / f(12.0) - f(0.5)) * scaled + f(0.625)) * scaled + f(5.0 / 3.0)) * scaled - f(5.0)) * scaled
        + f(4.0)
        - f(2.0) / (f(3.0) * scaled)
    )
    table = np.where(scaled <= 1.0, inside, np.where(scaled <= 2.0, outside, f(0.0))).astype(np.float32)
    return jnp.asarray(table / f(K - 1))


def lon_halo(cells, depth):
    nlon = lax.axis_size("lon")
    west = lax.ppermute(cells[:, -depth:], "lon", [(i, (i + 1) % nlon) for i in range(nlon)])
    east = lax.ppermute(cells[:, :depth], "lon", [((i + 1) % nlon, i) for i in range(nlon)])
    return jnp.concatenate([west, cells, east], axis=1), west, east


def lat_halo(first_row, last_row):
    nlat = lax.axis_size("lat")
    north = lax.ppermute(last_row, "lat", [(i, i + 1) for i in range(nlat - 1)])
    south = lax.ppermute(first_row, "lat", [(i + 1, i) for i in range(nlat - 1)])
    return north, south


def rows_kernel(
    plan, field_at, with_partial, target_off, emit, copies, tiles, targets_ref, edges_ref, taper_ref, *rest
):
    count = 1 + 2 * len(emit) + len(copies) + (tiles == "save")
    outs = rest[-count:]
    rest = rest[: len(rest) - count]
    out_ref = outs[0]
    partial_ref = rest[0] if with_partial else None
    sources = rest[1:] if with_partial else rest
    tiles_ref = outs[-1] if tiles == "save" else (sources[-1] if tiles == "load" else None)
    for (source, first, end), copy_ref in zip(copies, outs[1 + 2 * len(emit) :]):
        copy_ref[...] = sources[source][:, first:end, :K, :]
    columns, rank = out_ref.shape[2:]
    lat_blocks = out_ref.shape[0]
    lon_blocks = partial_ref.shape[1] if emit else out_ref.shape[1]
    for p in range(lat_blocks):

        def one_block(q, carry, p=p, uses=plan[p], side=None, middle=False):
            if side is None:
                target = targets_ref[p, q + target_off]
            else:
                target = edges_ref[p, side]
            if with_partial:
                total = partial_ref[p, q]
            else:
                total = jnp.zeros((columns, rank), jnp.float32)
            for dr, members_at, members_row, field_from, row, members_off, field_off, trim in uses:
                members_ref, field_ref = sources[members_at], sources[field_from]
                for dc in range(3):
                    slot = 3 * uses.index((dr, members_at, members_row, field_from, row, members_off, field_off, trim)) + dc
                    if tiles == "load":
                        tile_high = tiles_ref[p, q, slot, :columns, :]
                        tile_low = tiles_ref[p, q, slot, columns:, :]
                    else:
                        gram = jnp.dot(
                            target,
                            members_ref[members_row, q + dc + members_off, :K, :],
                            preferred_element_type=jnp.float32,
                        )
                        tile = gram * taper_ref[dr * 3 + dc]
                        tile_high = tile.astype(jnp.bfloat16)
                        tile_low = (tile - tile_high.astype(jnp.float32)).astype(jnp.bfloat16)
                        if tiles == "save" and middle:
                            tiles_ref[p, q - 1, slot, :columns, :] = tile_high
                            tiles_ref[p, q - 1, slot, columns:, :] = tile_low
                    partner = field_ref.at[row, q + dc + field_off]
                    if trim:
                        kept = columns - STRIDE
                        pad = jnp.zeros((STRIDE, rank), jnp.bfloat16)
                        field_high = partner[field_at : field_at + kept, :]
                        field_low = partner[field_at + kept : field_at + 2 * kept, :]
                        if trim == 1:
                            field_high = jnp.concatenate([pad, field_high], axis=0)
                            field_low = jnp.concatenate([pad, field_low], axis=0)
                        else:
                            field_high = jnp.concatenate([field_high, pad], axis=0)
                            field_low = jnp.concatenate([field_low, pad], axis=0)
                    else:
                        field_high = partner[field_at : field_at + columns, :]
                        field_low = partner[field_at + columns : field_at + 2 * columns, :]
                    total = total + jnp.dot(tile_high, field_high, preferred_element_type=jnp.float32)
                    total = total + jnp.dot(tile_high, field_low, preferred_element_type=jnp.float32)
                    total = total + jnp.dot(tile_low, field_high, preferred_element_type=jnp.float32)
            if emit:
                inner = out_ref.shape[1]
                shift = (lon_blocks - inner) // 2

                @pl.when((q >= shift) & (q < shift + inner))
                def _():
                    out_ref[p, jnp.clip(q - shift, 0, inner - 1)] = total

                high = total.astype(jnp.bfloat16)
                low = (total - high.astype(jnp.float32)).astype(jnp.bfloat16)
                row_ref = outs[1 + emit[p]]
                row_ref[0, q, :columns, :] = high
                row_ref[0, q, columns:, :] = low
                kept = columns - STRIDE
                sent_ref = outs[1 + len(emit) + emit[p]]
                if p == 0:
                    sent_ref[0, q, :kept, :] = high[:kept]
                    sent_ref[0, q, kept:, :] = low[:kept]
                else:
                    sent_ref[0, q, :kept, :] = high[STRIDE:]
                    sent_ref[0, q, kept:, :] = low[STRIDE:]
            else:
                out_ref[p, q] = total
            return carry

        if edges_ref is None:
            lax.fori_loop(0, lon_blocks, one_block, 0)
        else:
            one_block(0, 0, side=0)
            lax.fori_loop(1, lon_blocks - 1, functools.partial(one_block, middle=True), 0)
            one_block(lon_blocks - 1, 0, side=1)


def kernel_with_edges(*args):
    return rows_kernel(*args)


def kernel_without_edges(plan, field_at, with_partial, target_off, emit, copies, tiles, targets_ref, *rest):
    return rows_kernel(plan, field_at, with_partial, target_off, emit, copies, tiles, targets_ref, None, *rest)


def rows_call(
    plan,
    field_at,
    targets,
    taper,
    partial,
    sources,
    out_like,
    target_off=0,
    emit=(),
    edges=None,
    copies=(),
    tiles=None,
):
    lat_blocks, lon_blocks, columns, rank = (partial if emit else out_like).shape
    codes = sum(3 * len(uses) for uses in plan)
    flops = lon_blocks * codes * 2 * columns * (K * columns + 3 * columns * rank)
    operands = [targets] + ([edges] if edges is not None else []) + [taper]
    operands += ([partial] if partial is not None else []) + list(sources)
    shapes = [jax.ShapeDtypeStruct(out_like.shape, jnp.float32)]
    if emit:
        shapes += [jax.ShapeDtypeStruct((1, lon_blocks, 2 * columns, rank), jnp.bfloat16)] * len(emit)
        shapes += [jax.ShapeDtypeStruct((1, lon_blocks, 2 * (columns - STRIDE), rank), jnp.bfloat16)] * len(emit)
    for source, first, end in copies:
        held = sources[source]
        shapes.append(jax.ShapeDtypeStruct((held.shape[0], end - first, K, held.shape[3]), held.dtype))
    if tiles == "save":
        slots = max(3 * len(uses) for uses in plan)
        inner = lon_blocks - 2
        shapes.append(jax.ShapeDtypeStruct((lat_blocks, inner, slots, 2 * columns, rank), jnp.bfloat16))
    several = len(shapes) > 1
    moved = sum(x.size * x.dtype.itemsize for x in operands + shapes)
    vmem = pl.BlockSpec(memory_space=pltpu.VMEM)
    result = pl.pallas_call(
        functools.partial(
            kernel_with_edges if edges is not None else kernel_without_edges,
            plan,
            field_at,
            partial is not None,
            target_off,
            emit,
            copies,
            tiles,
        ),
        out_shape=tuple(shapes) if several else shapes[0],
        in_specs=[vmem] * len(operands),
        out_specs=tuple([vmem] * len(shapes)) if several else vmem,
        cost_estimate=pl.CostEstimate(flops=flops, bytes_accessed=moved, transcendentals=0),
    )(*operands)
    return result


def split_high_low(field):
    rounded = lax.reduce_precision(field, exponent_bits=8, mantissa_bits=7)
    return rounded.astype(jnp.bfloat16), (field - rounded).astype(jnp.bfloat16)


def own_plan(lat_blocks, members, fields, offsets):
    return tuple(
        tuple(
            (dr, members, p + dr - 1, fields[p + dr - 1], p + dr - 1 if len(set(fields)) == 1 else 0)
            + offsets
            + (0,)
            for dr in range(3)
            if 0 <= p + dr - 1 < lat_blocks
        )
        for p in range(lat_blocks)
    )


def halo_plan(lat_blocks, members, field, offsets, trimmed=False):
    return tuple(
        tuple(
            (dr, members[p + dr > 0], 0, field[p + dr > 0], 0)
            + offsets
            + ((1 if p + dr == 0 else 2) if trimmed else 0,)
            for dr in range(3)
            if not 0 <= p + dr - 1 < lat_blocks
        )
        for p in range(lat_blocks)
    )


def local(anomalies, panel, pair_code, pair_offset):
    del pair_code, pair_offset
    lat_blocks, lon_blocks = anomalies.shape[:2]
    taper = taper_by_code()
    panel_high, panel_low = split_high_low(panel)
    wider, west, east = lon_halo(jnp.concatenate([anomalies, panel_high, panel_low], axis=2), 2)
    kept = COLS - STRIDE
    going_north = jnp.concatenate(
        [wider[:1, :, :K], wider[:1, :, K : K + kept], wider[:1, :, K + COLS : K + COLS + kept]], axis=2
    )
    going_south = jnp.concatenate(
        [wider[-1:, :, :K], wider[-1:, :, K + STRIDE : K + COLS], wider[-1:, :, K + COLS + STRIDE :]], axis=2
    )
    north, south = lat_halo(going_north, going_south)
    targets = jnp.swapaxes(anomalies, 2, 3)
    edges = jnp.swapaxes(jnp.concatenate([west[:, 1:, :K, :], east[:, :1, :K, :]], axis=1), 2, 3)
    like_wide = jax.ShapeDtypeStruct((lat_blocks, lon_blocks + 2) + panel.shape[2:], jnp.float32)
    own_fields = (0,) * lat_blocks
    span = (1, lon_blocks + 3)
    partial, members, own_tiles = rows_call(
        own_plan(lat_blocks, 0, own_fields, (0, 0)),
        K,
        targets,
        taper,
        None,
        (wider,),
        like_wide,
        target_off=-1,
        edges=edges,
        copies=((0,) + span,),
        tiles="save",
    )
    emit = tuple(0 if p == 0 else 1 for p in range(lat_blocks))
    first_product, first_row, last_row, sent_north, sent_south, members_north, members_south = rows_call(
        halo_plan(lat_blocks, (0, 1), (0, 1), (0, 0), trimmed=True),
        K,
        targets,
        taper,
        partial,
        (north, south),
        panel,
        target_off=-1,
        emit=emit,
        edges=edges,
        copies=((0,) + span, (1,) + span),
    )
    north2, south2 = lat_halo(sent_north, sent_south)
    row_fields = (1, 2) if lat_blocks == 2 else None
    partial = rows_call(
        own_plan(lat_blocks, 0, row_fields, (0, 0)),
        0,
        targets,
        taper,
        None,
        (members, first_row, last_row, own_tiles),
        panel,
        tiles="load",
    )
    second_product = rows_call(
        halo_plan(lat_blocks, (0, 1), (2, 3), (0, 0), trimmed=True),
        0,
        targets,
        taper,
        partial,
        (members_north, members_south, north2, south2),
        panel,
    )
    return (first_product, second_product)


def solution(mesh):
    placed = (
        P("lat", "lon", None, None),
        P("lat", "lon", None, None),
        P("lat", "lon", None),
        P(None, "lat", "lon", None),
    )
    return jax.shard_map(
        local,
        mesh=mesh,
        in_specs=placed,
        out_specs=(P("lat", "lon", None, None), P("lat", "lon", None, None)),
        check_vma=False,
    )
```

```python
import functools

import numpy as np

import jax
import jax.numpy as jnp
from jax import lax
from jax.experimental import pallas as pl
from jax.experimental.pallas import tpu as pltpu
from jax.sharding import PartitionSpec as P

K = 80
COLS = 128
STRIDE = 16
RADIUS = 4
CODES = 9


def taper_by_code():
    codes = np.arange(CODES)
    shift_rows = ((codes // 3 - 1) * (COLS // STRIDE))[:, None, None]
    shift_cols = ((codes % 3 - 1) * STRIDE)[:, None, None]
    position = np.arange(COLS)
    row_within = position // STRIDE
    col_within = position % STRIDE
    delta_rows = shift_rows + (row_within[None, :] - row_within[:, None])
    delta_cols = shift_cols + (col_within[None, :] - col_within[:, None])
    squared = (delta_rows * delta_rows + delta_cols * delta_cols).astype(np.float32)
    f = np.float32
    scaled = np.sqrt(squared + f(0.25)) / f(RADIUS)
    inside = (
        ((f(-0.25) * scaled + f(0.5)) * scaled + f(0.625)) * scaled - f(5.0 / 3.0)
    ) * scaled * scaled + f(1.0)
    outside = (
        ((((scaled / f(12.0) - f(0.5)) * scaled + f(0.625)) * scaled + f(5.0 / 3.0)) * scaled - f(5.0)) * scaled
        + f(4.0)
        - f(2.0) / (f(3.0) * scaled)
    )
    table = np.where(scaled <= 1.0, inside, np.where(scaled <= 2.0, outside, f(0.0))).astype(np.float32)
    return jnp.asarray(table / f(K - 1))


def lon_halo(cells, depth):
    nlon = lax.axis_size("lon")
    west = lax.ppermute(cells[:, -depth:], "lon", [(i, (i + 1) % nlon) for i in range(nlon)])
    east = lax.ppermute(cells[:, :depth], "lon", [((i + 1) % nlon, i) for i in range(nlon)])
    return jnp.concatenate([west, cells, east], axis=1), west, east


def lat_halo(first_row, last_row):
    nlat = lax.axis_size("lat")
    north = lax.ppermute(last_row, "lat", [(i, i + 1) for i in range(nlat - 1)])
    south = lax.ppermute(first_row, "lat", [(i + 1, i) for i in range(nlat - 1)])
    return north, south


def rows_kernel(
    plan, field_at, with_partial, target_off, emit, copies, tiles, targets_ref, edges_ref, taper_ref, *rest
):
    count = 1 + 2 * len(emit) + len(copies) + (tiles == "save")
    outs = rest[-count:]
    rest = rest[: len(rest) - count]
    out_ref = outs[0]
    partial_ref = rest[0] if with_partial else None
    sources = rest[1:] if with_partial else rest
    tiles_ref = outs[-1] if tiles == "save" else (sources[-1] if tiles == "load" else None)
    for (source, first, end), copy_ref in zip(copies, outs[1 + 2 * len(emit) :]):
        copy_ref[...] = sources[source][:, first:end, :K, :]
    columns, rank = out_ref.shape[2:]
    lat_blocks = out_ref.shape[0]
    lon_blocks = partial_ref.shape[1] if emit else out_ref.shape[1]
    for p in range(lat_blocks):

        def one_block(q, carry, p=p, uses=plan[p], side=None, middle=False):
            if side is None:
                target = targets_ref[p, q + target_off]
            else:
                target = edges_ref[p, side]
            if with_partial:
                total = partial_ref[p, q]
            else:
                total = jnp.zeros((columns, rank), jnp.float32)
            for dr, members_at, members_row, field_from, row, members_off, field_off, trim in uses:
                members_ref, field_ref = sources[members_at], sources[field_from]
                for dc in range(3):
                    slot = 3 * uses.index((dr, members_at, members_row, field_from, row, members_off, field_off, trim)) + dc
                    if tiles == "load":
                        tile_high = tiles_ref[p, q, slot, :columns, :]
                        tile_low = tiles_ref[p, q, slot, columns:, :]
                    else:
                        gram = jnp.dot(
                            target,
                            members_ref[members_row, q + dc + members_off, :K, :],
                            preferred_element_type=jnp.float32,
                        )
                        tile = gram * taper_ref[dr * 3 + dc]
                        tile_high = tile.astype(jnp.bfloat16)
                        tile_low = (tile - tile_high.astype(jnp.float32)).astype(jnp.bfloat16)
                        if tiles == "save" and middle:
                            tiles_ref[p, q - 1, slot, :columns, :] = tile_high
                            tiles_ref[p, q - 1, slot, columns:, :] = tile_low
                    partner = field_ref.at[row, q + dc + field_off]
                    if trim:
                        kept = columns - STRIDE
                        pad = jnp.zeros((STRIDE, rank), jnp.bfloat16)
                        field_high = partner[field_at : field_at + kept, :]
                        field_low = partner[field_at + kept : field_at + 2 * kept, :]
                        if trim == 1:
                            field_high = jnp.concatenate([pad, field_high], axis=0)
                            field_low = jnp.concatenate([pad, field_low], axis=0)
                        else:
                            field_high = jnp.concatenate([field_high, pad], axis=0)
                            field_low = jnp.concatenate([field_low, pad], axis=0)
                    else:
                        field_high = partner[field_at : field_at + columns, :]
                        field_low = partner[field_at + columns : field_at + 2 * columns, :]
                    total = total + jnp.dot(tile_high, field_high, preferred_element_type=jnp.float32)
                    total = total + jnp.dot(tile_high, field_low, preferred_element_type=jnp.float32)
                    total = total + jnp.dot(tile_low, field_high, preferred_element_type=jnp.float32)
            if emit:
                inner = out_ref.shape[1]
                shift = (lon_blocks - inner) // 2

                @pl.when((q >= shift) & (q < shift + inner))
                def _():
                    out_ref[p, jnp.clip(q - shift, 0, inner - 1)] = total

                high = total.astype(jnp.bfloat16)
                low = (total - high.astype(jnp.float32)).astype(jnp.bfloat16)
                row_ref = outs[1 + emit[p]]
                row_ref[0, q, :columns, :] = high
                row_ref[0, q, columns:, :] = low
                kept = columns - STRIDE
                sent_ref = outs[1 + len(emit) + emit[p]]
                if p == 0:
                    sent_ref[0, q, :kept, :] = high[:kept]
                    sent_ref[0, q, kept:, :] = low[:kept]
                else:
                    sent_ref[0, q, :kept, :] = high[STRIDE:]
                    sent_ref[0, q, kept:, :] = low[STRIDE:]
            else:
                out_ref[p, q] = total
            return carry

        if edges_ref is None:
            lax.fori_loop(0, lon_blocks, one_block, 0)
        else:
            one_block(0, 0, side=0)
            lax.fori_loop(1, lon_blocks - 1, functools.partial(one_block, middle=True), 0)
            one_block(lon_blocks - 1, 0, side=1)


def kernel_with_edges(*args):
    return rows_kernel(*args)


def kernel_without_edges(plan, field_at, with_partial, target_off, emit, copies, tiles, targets_ref, *rest):
    return rows_kernel(plan, field_at, with_partial, target_off, emit, copies, tiles, targets_ref, None, *rest)


def rows_call(
    plan,
    field_at,
    targets,
    taper,
    partial,
    sources,
    out_like,
    target_off=0,
    emit=(),
    edges=None,
    copies=(),
    tiles=None,
):
    lat_blocks, lon_blocks, columns, rank = (partial if emit else out_like).shape
    codes = sum(3 * len(uses) for uses in plan)
    flops = lon_blocks * codes * 2 * columns * (K * columns + 3 * columns * rank)
    operands = [targets] + ([edges] if edges is not None else []) + [taper]
    operands += ([partial] if partial is not None else []) + list(sources)
    shapes = [jax.ShapeDtypeStruct(out_like.shape, jnp.float32)]
    if emit:
        shapes += [jax.ShapeDtypeStruct((1, lon_blocks, 2 * columns, rank), jnp.bfloat16)] * len(emit)
        shapes += [jax.ShapeDtypeStruct((1, lon_blocks, 2 * (columns - STRIDE), rank), jnp.bfloat16)] * len(emit)
    for source, first, end in copies:
        held = sources[source]
        shapes.append(jax.ShapeDtypeStruct((held.shape[0], end - first, K, held.shape[3]), held.dtype))
    if tiles == "save":
        slots = max(3 * len(uses) for uses in plan)
        inner = lon_blocks - 2
        shapes.append(jax.ShapeDtypeStruct((lat_blocks, inner, slots, 2 * columns, rank), jnp.bfloat16))
    several = len(shapes) > 1
    moved = sum(x.size * x.dtype.itemsize for x in operands + shapes)
    vmem = pl.BlockSpec(memory_space=pltpu.VMEM)
    result = pl.pallas_call(
        functools.partial(
            kernel_with_edges if edges is not None else kernel_without_edges,
            plan,
            field_at,
            partial is not None,
            target_off,
            emit,
            copies,
            tiles,
        ),
        out_shape=tuple(shapes) if several else shapes[0],
        in_specs=[vmem] * len(operands),
        out_specs=tuple([vmem] * len(shapes)) if several else vmem,
        cost_estimate=pl.CostEstimate(flops=flops, bytes_accessed=moved, transcendentals=0),
    )(*operands)
    return result


def split_high_low(field):
    rounded = lax.reduce_precision(field, exponent_bits=8, mantissa_bits=7)
    return rounded.astype(jnp.bfloat16), (field - rounded).astype(jnp.bfloat16)


def own_plan(lat_blocks, members, fields, offsets):
    return tuple(
        tuple(
            (dr, members, p + dr - 1, fields[p + dr - 1], p + dr - 1 if len(set(fields)) == 1 else 0)
            + offsets
            + (0,)
            for dr in range(3)
            if 0 <= p + dr - 1 < lat_blocks
        )
        for p in range(lat_blocks)
    )


def halo_plan(lat_blocks, members, field, offsets, trimmed=False):
    return tuple(
        tuple(
            (dr, members[p + dr > 0], 0, field[p + dr > 0], 0)
            + offsets
            + ((1 if p + dr == 0 else 2) if trimmed else 0,)
            for dr in range(3)
            if not 0 <= p + dr - 1 < lat_blocks
        )
        for p in range(lat_blocks)
    )


def local(anomalies, panel, pair_code, pair_offset):
    del pair_code, pair_offset
    lat_blocks, lon_blocks = anomalies.shape[:2]
    taper = taper_by_code()
    panel_high, panel_low = split_high_low(panel)
    wider, west, east = lon_halo(jnp.concatenate([anomalies, panel_high, panel_low], axis=2), 2)
    kept = COLS - STRIDE
    going_north = jnp.concatenate(
        [wider[:1, :, :K], wider[:1, :, K : K + kept], wider[:1, :, K + COLS : K + COLS + kept]], axis=2
    )
    going_south = jnp.concatenate(
        [wider[-1:, :, :K], wider[-1:, :, K + STRIDE : K + COLS], wider[-1:, :, K + COLS + STRIDE :]], axis=2
    )
    north, south = lat_halo(going_north, going_south)
    targets = jnp.swapaxes(anomalies, 2, 3)
    edges = jnp.swapaxes(jnp.concatenate([west[:, 1:, :K, :], east[:, :1, :K, :]], axis=1), 2, 3)
    like_wide = jax.ShapeDtypeStruct((lat_blocks, lon_blocks + 2) + panel.shape[2:], jnp.float32)
    own_fields = (0,) * lat_blocks
    span = (1, lon_blocks + 3)
    partial, members, own_tiles = rows_call(
        own_plan(lat_blocks, 0, own_fields, (0, 0)),
        K,
        targets,
        taper,
        None,
        (wider,),
        like_wide,
        target_off=-1,
        edges=edges,
        copies=((0,) + span,),
        tiles="save",
    )
    emit = tuple(0 if p == 0 else 1 for p in range(lat_blocks))
    first_product, first_row, last_row, sent_north, sent_south, members_north, members_south, halo_tiles = rows_call(
        halo_plan(lat_blocks, (0, 1), (0, 1), (0, 0), trimmed=True),
        K,
        targets,
        taper,
        partial,
        (north, south),
        panel,
        target_off=-1,
        emit=emit,
        edges=edges,
        copies=((0,) + span, (1,) + span),
        tiles="save",
    )
    north2, south2 = lat_halo(sent_north, sent_south)
    row_fields = (1, 2) if lat_blocks == 2 else None
    partial = rows_call(
        own_plan(lat_blocks, 0, row_fields, (0, 0)),
        0,
        targets,
        taper,
        None,
        (members, first_row, last_row, own_tiles),
        panel,
        tiles="load",
    )
    second_product = rows_call(
        halo_plan(lat_blocks, (0, 1), (2, 3), (0, 0), trimmed=True),
        0,
        targets,
        taper,
        partial,
        (members_north, members_south, north2, south2, halo_tiles),
        panel,
        tiles="load",
    )
    return (first_product, second_product)


def solution(mesh):
    placed = (
        P("lat", "lon", None, None),
        P("lat", "lon", None, None),
        P("lat", "lon", None),
        P(None, "lat", "lon", None),
    )
    return jax.shard_map(
        local,
        mesh=mesh,
        in_specs=placed,
        out_specs=(P("lat", "lon", None, None), P("lat", "lon", None, None)),
        check_vma=False,
    )
```

```python
import functools

import numpy as np

import jax
import jax.numpy as jnp
from jax import lax
from jax.experimental import pallas as pl
from jax.experimental.pallas import tpu as pltpu
from jax.sharding import PartitionSpec as P

K = 80
COLS = 128
STRIDE = 16
RADIUS = 4
CODES = 9


def taper_by_code():
    codes = np.arange(CODES)
    shift_rows = ((codes // 3 - 1) * (COLS // STRIDE))[:, None, None]
    shift_cols = ((codes % 3 - 1) * STRIDE)[:, None, None]
    position = np.arange(COLS)
    row_within = position // STRIDE
    col_within = position % STRIDE
    delta_rows = shift_rows + (row_within[None, :] - row_within[:, None])
    delta_cols = shift_cols + (col_within[None, :] - col_within[:, None])
    squared = (delta_rows * delta_rows + delta_cols * delta_cols).astype(np.float32)
    f = np.float32
    scaled = np.sqrt(squared + f(0.25)) / f(RADIUS)
    inside = (
        ((f(-0.25) * scaled + f(0.5)) * scaled + f(0.625)) * scaled - f(5.0 / 3.0)
    ) * scaled * scaled + f(1.0)
    outside = (
        ((((scaled / f(12.0) - f(0.5)) * scaled + f(0.625)) * scaled + f(5.0 / 3.0)) * scaled - f(5.0)) * scaled
        + f(4.0)
        - f(2.0) / (f(3.0) * scaled)
    )
    table = np.where(scaled <= 1.0, inside, np.where(scaled <= 2.0, outside, f(0.0))).astype(np.float32)
    return jnp.asarray(table / f(K - 1))


def lon_halo(cells, depth):
    nlon = lax.axis_size("lon")
    west = lax.ppermute(cells[:, -depth:], "lon", [(i, (i + 1) % nlon) for i in range(nlon)])
    east = lax.ppermute(cells[:, :depth], "lon", [((i + 1) % nlon, i) for i in range(nlon)])
    return jnp.concatenate([west, cells, east], axis=1), west, east


def lat_halo(first_row, last_row):
    nlat = lax.axis_size("lat")
    north = lax.ppermute(last_row, "lat", [(i, i + 1) for i in range(nlat - 1)])
    south = lax.ppermute(first_row, "lat", [(i + 1, i) for i in range(nlat - 1)])
    return north, south


def rows_kernel(
    plan, field_at, with_partial, target_off, emit, copies, tiles, extra, targets_ref, edges_ref, taper_ref, *rest
):
    count = 1 + 2 * len(emit) + len(copies) + (tiles == "save") + bool(extra)
    outs = rest[-count:]
    rest = rest[: len(rest) - count]
    out_ref = outs[0]
    partial_ref = rest[0] if with_partial else None
    sources = rest[1:] if with_partial else rest
    tiles_ref = outs[-1] if tiles == "save" else (sources[-1] if tiles == "load" else None)
    extra_ref = outs[-1] if extra else None
    for (source, first, end), copy_ref in zip(copies, outs[1 + 2 * len(emit) :]):
        copy_ref[...] = sources[source][:, first:end, :K, :]
    columns, rank = out_ref.shape[2:]
    lat_blocks = out_ref.shape[0]
    lon_blocks = partial_ref.shape[1] if emit else out_ref.shape[1]
    for p in range(lat_blocks):

        def one_block(q, carry, p=p, uses=plan[p], side=None, middle=False):
            if side is None:
                target = targets_ref[p, q + target_off]
            else:
                target = edges_ref[p, side]
            if with_partial:
                total = partial_ref[p, q]
            else:
                total = jnp.zeros((columns, rank), jnp.float32)
            for dr, members_at, members_row, field_from, row, members_off, field_off, trim in uses:
                members_ref, field_ref = sources[members_at], sources[field_from]
                for dc in range(3):
                    slot = 3 * uses.index((dr, members_at, members_row, field_from, row, members_off, field_off, trim)) + dc
                    if tiles == "load":
                        tile_high = tiles_ref[p, q, slot, :columns, :]
                        tile_low = tiles_ref[p, q, slot, columns:, :]
                    else:
                        gram = jnp.dot(
                            target,
                            members_ref[members_row, q + dc + members_off, :K, :],
                            preferred_element_type=jnp.float32,
                        )
                        tile = gram * taper_ref[dr * 3 + dc]
                        tile_high = tile.astype(jnp.bfloat16)
                        tile_low = (tile - tile_high.astype(jnp.float32)).astype(jnp.bfloat16)
                        if tiles == "save" and middle:
                            tiles_ref[p, q - 1, slot, :columns, :] = tile_high
                            tiles_ref[p, q - 1, slot, columns:, :] = tile_low
                    partner = field_ref.at[row, q + dc + field_off]
                    if trim:
                        kept = columns - STRIDE
                        pad = jnp.zeros((STRIDE, rank), jnp.bfloat16)
                        field_high = partner[field_at : field_at + kept, :]
                        field_low = partner[field_at + kept : field_at + 2 * kept, :]
                        if trim == 1:
                            field_high = jnp.concatenate([pad, field_high], axis=0)
                            field_low = jnp.concatenate([pad, field_low], axis=0)
                        else:
                            field_high = jnp.concatenate([field_high, pad], axis=0)
                            field_low = jnp.concatenate([field_low, pad], axis=0)
                    else:
                        field_high = partner[field_at : field_at + columns, :]
                        field_low = partner[field_at + columns : field_at + 2 * columns, :]
                    total = total + jnp.dot(tile_high, field_high, preferred_element_type=jnp.float32)
                    total = total + jnp.dot(tile_high, field_low, preferred_element_type=jnp.float32)
                    total = total + jnp.dot(tile_low, field_high, preferred_element_type=jnp.float32)
            for index, (dr, members_at, members_row, _, _, members_off, _, _) in enumerate(extra[p] if extra else ()):
                for dc in range(3):
                    gram = jnp.dot(
                        target,
                        sources[members_at][members_row, q + dc + members_off, :K, :],
                        preferred_element_type=jnp.float32,
                    )
                    tile = gram * taper_ref[dr * 3 + dc]
                    tile_high = tile.astype(jnp.bfloat16)
                    tile_low = (tile - tile_high.astype(jnp.float32)).astype(jnp.bfloat16)
                    extra_ref[p, q, 3 * index + dc, :columns, :] = tile_high
                    extra_ref[p, q, 3 * index + dc, columns:, :] = tile_low
            if emit:
                inner = out_ref.shape[1]
                shift = (lon_blocks - inner) // 2

                @pl.when((q >= shift) & (q < shift + inner))
                def _():
                    out_ref[p, jnp.clip(q - shift, 0, inner - 1)] = total

                high = total.astype(jnp.bfloat16)
                low = (total - high.astype(jnp.float32)).astype(jnp.bfloat16)
                row_ref = outs[1 + emit[p]]
                row_ref[0, q, :columns, :] = high
                row_ref[0, q, columns:, :] = low
                kept = columns - STRIDE
                sent_ref = outs[1 + len(emit) + emit[p]]
                if p == 0:
                    sent_ref[0, q, :kept, :] = high[:kept]
                    sent_ref[0, q, kept:, :] = low[:kept]
                else:
                    sent_ref[0, q, :kept, :] = high[STRIDE:]
                    sent_ref[0, q, kept:, :] = low[STRIDE:]
            else:
                out_ref[p, q] = total
            return carry

        if edges_ref is None:
            lax.fori_loop(0, lon_blocks, one_block, 0)
        else:
            one_block(0, 0, side=0)
            lax.fori_loop(1, lon_blocks - 1, functools.partial(one_block, middle=True), 0)
            one_block(lon_blocks - 1, 0, side=1)


def kernel_with_edges(*args):
    return rows_kernel(*args)


def kernel_without_edges(plan, field_at, with_partial, target_off, emit, copies, tiles, extra, targets_ref, *rest):
    return rows_kernel(plan, field_at, with_partial, target_off, emit, copies, tiles, extra, targets_ref, None, *rest)


def rows_call(
    plan,
    field_at,
    targets,
    taper,
    partial,
    sources,
    out_like,
    target_off=0,
    emit=(),
    edges=None,
    copies=(),
    tiles=None,
    extra=(),
):
    lat_blocks, lon_blocks, columns, rank = (partial if emit else out_like).shape
    codes = sum(3 * len(uses) for uses in plan)
    flops = lon_blocks * codes * 2 * columns * (K * columns + 3 * columns * rank)
    operands = [targets] + ([edges] if edges is not None else []) + [taper]
    operands += ([partial] if partial is not None else []) + list(sources)
    shapes = [jax.ShapeDtypeStruct(out_like.shape, jnp.float32)]
    if emit:
        shapes += [jax.ShapeDtypeStruct((1, lon_blocks, 2 * columns, rank), jnp.bfloat16)] * len(emit)
        shapes += [jax.ShapeDtypeStruct((1, lon_blocks, 2 * (columns - STRIDE), rank), jnp.bfloat16)] * len(emit)
    for source, first, end in copies:
        held = sources[source]
        shapes.append(jax.ShapeDtypeStruct((held.shape[0], end - first, K, held.shape[3]), held.dtype))
    if tiles == "save":
        slots = max(3 * len(uses) for uses in plan)
        inner = lon_blocks - 2
        shapes.append(jax.ShapeDtypeStruct((lat_blocks, inner, slots, 2 * columns, rank), jnp.bfloat16))
    if extra:
        slots = max(3 * len(uses) for uses in extra)
        shapes.append(jax.ShapeDtypeStruct((lat_blocks, lon_blocks, slots, 2 * columns, rank), jnp.bfloat16))
    several = len(shapes) > 1
    moved = sum(x.size * x.dtype.itemsize for x in operands + shapes)
    vmem = pl.BlockSpec(memory_space=pltpu.VMEM)
    result = pl.pallas_call(
        functools.partial(
            kernel_with_edges if edges is not None else kernel_without_edges,
            plan,
            field_at,
            partial is not None,
            target_off,
            emit,
            copies,
            tiles,
            extra,
        ),
        out_shape=tuple(shapes) if several else shapes[0],
        in_specs=[vmem] * len(operands),
        out_specs=tuple([vmem] * len(shapes)) if several else vmem,
        cost_estimate=pl.CostEstimate(flops=flops, bytes_accessed=moved, transcendentals=0),
    )(*operands)
    return result


def split_high_low(field):
    rounded = lax.reduce_precision(field, exponent_bits=8, mantissa_bits=7)
    return rounded.astype(jnp.bfloat16), (field - rounded).astype(jnp.bfloat16)


def own_plan(lat_blocks, members, fields, offsets):
    return tuple(
        tuple(
            (dr, members, p + dr - 1, fields[p + dr - 1], p + dr - 1 if len(set(fields)) == 1 else 0)
            + offsets
            + (0,)
            for dr in range(3)
            if 0 <= p + dr - 1 < lat_blocks
        )
        for p in range(lat_blocks)
    )


def halo_plan(lat_blocks, members, field, offsets, trimmed=False):
    return tuple(
        tuple(
            (dr, members[p + dr > 0], 0, field[p + dr > 0], 0)
            + offsets
            + ((1 if p + dr == 0 else 2) if trimmed else 0,)
            for dr in range(3)
            if not 0 <= p + dr - 1 < lat_blocks
        )
        for p in range(lat_blocks)
    )


def local(anomalies, panel, pair_code, pair_offset):
    del pair_code, pair_offset
    lat_blocks, lon_blocks = anomalies.shape[:2]
    taper = taper_by_code()
    panel_high, panel_low = split_high_low(panel)
    wider, west, east = lon_halo(jnp.concatenate([anomalies, panel_high, panel_low], axis=2), 2)
    kept = COLS - STRIDE
    going_north = jnp.concatenate(
        [wider[:1, :, :K], wider[:1, :, K : K + kept], wider[:1, :, K + COLS : K + COLS + kept]], axis=2
    )
    going_south = jnp.concatenate(
        [wider[-1:, :, :K], wider[-1:, :, K + STRIDE : K + COLS], wider[-1:, :, K + COLS + STRIDE :]], axis=2
    )
    north, south = lat_halo(going_north, going_south)
    targets = jnp.swapaxes(anomalies, 2, 3)
    edges = jnp.swapaxes(jnp.concatenate([west[:, 1:, :K, :], east[:, :1, :K, :]], axis=1), 2, 3)
    like_wide = jax.ShapeDtypeStruct((lat_blocks, lon_blocks + 2) + panel.shape[2:], jnp.float32)
    own_fields = (0,) * lat_blocks
    span = (1, lon_blocks + 3)
    partial, members, own_tiles = rows_call(
        own_plan(lat_blocks, 0, own_fields, (0, 0)),
        K,
        targets,
        taper,
        None,
        (wider,),
        like_wide,
        target_off=-1,
        edges=edges,
        copies=((0,) + span,),
        tiles="save",
    )
    emit = tuple(0 if p == 0 else 1 for p in range(lat_blocks))
    first_product, first_row, last_row, sent_north, sent_south, members_north, members_south = rows_call(
        halo_plan(lat_blocks, (0, 1), (0, 1), (0, 0), trimmed=True),
        K,
        targets,
        taper,
        partial,
        (north, south),
        panel,
        target_off=-1,
        emit=emit,
        edges=edges,
        copies=((0,) + span, (1,) + span),
    )
    north2, south2 = lat_halo(sent_north, sent_south)
    row_fields = (1, 2) if lat_blocks == 2 else None
    partial, halo_tiles = rows_call(
        own_plan(lat_blocks, 0, row_fields, (0, 0)),
        0,
        targets,
        taper,
        None,
        (members, first_row, last_row, members_north, members_south, own_tiles),
        panel,
        tiles="load",
        extra=halo_plan(lat_blocks, (3, 4), (3, 4), (0, 0)),
    )
    second_product = rows_call(
        halo_plan(lat_blocks, (0, 1), (2, 3), (0, 0), trimmed=True),
        0,
        targets,
        taper,
        partial,
        (members_north, members_south, north2, south2, halo_tiles),
        panel,
        tiles="load",
    )
    return (first_product, second_product)


def solution(mesh):
    placed = (
        P("lat", "lon", None, None),
        P("lat", "lon", None, None),
        P("lat", "lon", None),
        P(None, "lat", "lon", None),
    )
    return jax.shard_map(
        local,
        mesh=mesh,
        in_specs=placed,
        out_specs=(P("lat", "lon", None, None), P("lat", "lon", None, None)),
        check_vma=False,
    )
```

```python
import functools

import numpy as np

import jax
import jax.numpy as jnp
from jax import lax
from jax.experimental import pallas as pl
from jax.experimental.pallas import tpu as pltpu
from jax.sharding import PartitionSpec as P

K = 80
COLS = 128
STRIDE = 16
RADIUS = 4
CODES = 9


def taper_by_code():
    codes = np.arange(CODES)
    shift_rows = ((codes // 3 - 1) * (COLS // STRIDE))[:, None, None]
    shift_cols = ((codes % 3 - 1) * STRIDE)[:, None, None]
    position = np.arange(COLS)
    row_within = position // STRIDE
    col_within = position % STRIDE
    delta_rows = shift_rows + (row_within[None, :] - row_within[:, None])
    delta_cols = shift_cols + (col_within[None, :] - col_within[:, None])
    squared = (delta_rows * delta_rows + delta_cols * delta_cols).astype(np.float32)
    f = np.float32
    scaled = np.sqrt(squared + f(0.25)) / f(RADIUS)
    inside = (
        ((f(-0.25) * scaled + f(0.5)) * scaled + f(0.625)) * scaled - f(5.0 / 3.0)
    ) * scaled * scaled + f(1.0)
    outside = (
        ((((scaled / f(12.0) - f(0.5)) * scaled + f(0.625)) * scaled + f(5.0 / 3.0)) * scaled - f(5.0)) * scaled
        + f(4.0)
        - f(2.0) / (f(3.0) * scaled)
    )
    table = np.where(scaled <= 1.0, inside, np.where(scaled <= 2.0, outside, f(0.0))).astype(np.float32)
    return jnp.asarray(table / f(K - 1))


def lon_halo(cells, depth):
    nlon = lax.axis_size("lon")
    west = lax.ppermute(cells[:, -depth:], "lon", [(i, (i + 1) % nlon) for i in range(nlon)])
    east = lax.ppermute(cells[:, :depth], "lon", [((i + 1) % nlon, i) for i in range(nlon)])
    return jnp.concatenate([west, cells, east], axis=1), west, east


def lat_halo(first_row, last_row):
    nlat = lax.axis_size("lat")
    north = lax.ppermute(last_row, "lat", [(i, i + 1) for i in range(nlat - 1)])
    south = lax.ppermute(first_row, "lat", [(i + 1, i) for i in range(nlat - 1)])
    return north, south


def rows_kernel(
    plan, field_at, with_partial, target_off, emit, copies, tiles, extra, targets_ref, edges_ref, taper_ref, *rest
):
    count = 1 + 2 * len(emit) + len(copies) + (tiles == "save") + bool(extra)
    outs = rest[-count:]
    rest = rest[: len(rest) - count]
    out_ref = outs[0]
    partial_ref = rest[0] if with_partial else None
    sources = rest[1:] if with_partial else rest
    tiles_ref = outs[-1] if tiles == "save" else (sources[-1] if tiles == "load" else None)
    extra_ref = outs[-1] if extra else None
    for (source, first, end), copy_ref in zip(copies, outs[1 + 2 * len(emit) :]):
        copy_ref[...] = sources[source][:, first:end, :K, :]
    columns, rank = out_ref.shape[2:]
    lat_blocks = out_ref.shape[0]
    lon_blocks = partial_ref.shape[1] if emit else out_ref.shape[1]
    for p in range(lat_blocks):

        def one_block(q, carry, p=p, uses=plan[p], side=None, middle=False):
            if side is None:
                target = targets_ref[p, q + target_off]
            else:
                target = edges_ref[p, side]
            if with_partial:
                total = partial_ref[p, q]
            else:
                total = jnp.zeros((columns, rank), jnp.float32)
            for dr, members_at, members_row, field_from, row, members_off, field_off, trim in uses:
                members_ref, field_ref = sources[members_at], sources[field_from]
                for dc in range(3):
                    slot = 3 * uses.index((dr, members_at, members_row, field_from, row, members_off, field_off, trim)) + dc
                    if tiles == "load":
                        tile_high = tiles_ref[p, q, slot, :columns, :]
                        tile_low = tiles_ref[p, q, slot, columns:, :]
                    else:
                        gram = jnp.dot(
                            target,
                            members_ref[members_row, q + dc + members_off, :K, :],
                            preferred_element_type=jnp.float32,
                        )
                        tile = gram * taper_ref[dr * 3 + dc]
                        tile_high = tile.astype(jnp.bfloat16)
                        tile_low = (tile - tile_high.astype(jnp.float32)).astype(jnp.bfloat16)
                        if tiles == "save" and middle:
                            tiles_ref[p, q - 1, slot, :columns, :] = tile_high
                            tiles_ref[p, q - 1, slot, columns:, :] = tile_low
                    partner = field_ref.at[row, q + dc + field_off]
                    if trim:
                        kept = columns - STRIDE
                        pad = jnp.zeros((STRIDE, rank), jnp.bfloat16)
                        field_high = partner[field_at : field_at + kept, :]
                        field_low = partner[field_at + kept : field_at + 2 * kept, :]
                        if trim == 1:
                            field_high = jnp.concatenate([pad, field_high], axis=0)
                            field_low = jnp.concatenate([pad, field_low], axis=0)
                        else:
                            field_high = jnp.concatenate([field_high, pad], axis=0)
                            field_low = jnp.concatenate([field_low, pad], axis=0)
                    else:
                        field_high = partner[field_at : field_at + columns, :]
                        field_low = partner[field_at + columns : field_at + 2 * columns, :]
                    total = total + jnp.dot(tile_high, field_high, preferred_element_type=jnp.float32)
                    total = total + jnp.dot(tile_high, field_low, preferred_element_type=jnp.float32)
                    total = total + jnp.dot(tile_low, field_high, preferred_element_type=jnp.float32)
            for index, (dr, members_at, members_row, _, _, members_off, _, _) in enumerate(extra[p] if extra else ()):
                for dc in range(3):
                    gram = jnp.dot(
                        target,
                        sources[members_at][members_row, q + dc + members_off, :K, :],
                        preferred_element_type=jnp.float32,
                    )
                    tile = gram * taper_ref[dr * 3 + dc]
                    tile_high = tile.astype(jnp.bfloat16)
                    tile_low = (tile - tile_high.astype(jnp.float32)).astype(jnp.bfloat16)
                    extra_ref[p, q, 3 * index + dc, :columns, :] = tile_high
                    extra_ref[p, q, 3 * index + dc, columns:, :] = tile_low
            if emit:
                inner = out_ref.shape[1]
                shift = (lon_blocks - inner) // 2

                @pl.when((q >= shift) & (q < shift + inner))
                def _():
                    out_ref[p, jnp.clip(q - shift, 0, inner - 1)] = total

                high = total.astype(jnp.bfloat16)
                low = (total - high.astype(jnp.float32)).astype(jnp.bfloat16)
                row_ref = outs[1 + emit[p]]
                row_ref[0, q, :columns, :] = high
                row_ref[0, q, columns:, :] = low
                kept = columns - STRIDE
                sent_ref = outs[1 + len(emit) + emit[p]]
                if p == 0:
                    sent_ref[0, q, :kept, :] = high[:kept]
                    sent_ref[0, q, kept:, :] = low[:kept]
                else:
                    sent_ref[0, q, :kept, :] = high[STRIDE:]
                    sent_ref[0, q, kept:, :] = low[STRIDE:]
            else:
                out_ref[p, q] = total
            return carry

        if edges_ref is None:
            lax.fori_loop(0, lon_blocks, one_block, 0)
        else:
            one_block(0, 0, side=0)
            lax.fori_loop(1, lon_blocks - 1, functools.partial(one_block, middle=True), 0)
            one_block(lon_blocks - 1, 0, side=1)


def kernel_with_edges(*args):
    return rows_kernel(*args)


def kernel_without_edges(plan, field_at, with_partial, target_off, emit, copies, tiles, extra, targets_ref, *rest):
    return rows_kernel(plan, field_at, with_partial, target_off, emit, copies, tiles, extra, targets_ref, None, *rest)


def rows_call(
    plan,
    field_at,
    targets,
    taper,
    partial,
    sources,
    out_like,
    target_off=0,
    emit=(),
    edges=None,
    copies=(),
    tiles=None,
    extra=(),
):
    lat_blocks, lon_blocks, columns, rank = (partial if emit else out_like).shape
    codes = sum(3 * len(uses) for uses in plan)
    flops = lon_blocks * codes * 2 * columns * (K * columns + 3 * columns * rank)
    operands = [targets] + ([edges] if edges is not None else []) + [taper]
    operands += ([partial] if partial is not None else []) + list(sources)
    shapes = [jax.ShapeDtypeStruct(out_like.shape, jnp.float32)]
    if emit:
        shapes += [jax.ShapeDtypeStruct((1, lon_blocks, 2 * columns, rank), jnp.bfloat16)] * len(emit)
        shapes += [jax.ShapeDtypeStruct((1, lon_blocks, 2 * (columns - STRIDE), rank), jnp.bfloat16)] * len(emit)
    for source, first, end in copies:
        held = sources[source]
        shapes.append(jax.ShapeDtypeStruct((held.shape[0], end - first, K, held.shape[3]), held.dtype))
    if tiles == "save":
        slots = max(3 * len(uses) for uses in plan)
        inner = lon_blocks - 2
        shapes.append(jax.ShapeDtypeStruct((lat_blocks, inner, slots, 2 * columns, rank), jnp.bfloat16))
    if extra:
        slots = max(3 * len(uses) for uses in extra)
        shapes.append(jax.ShapeDtypeStruct((lat_blocks, lon_blocks, slots, 2 * columns, rank), jnp.bfloat16))
    several = len(shapes) > 1
    moved = sum(x.size * x.dtype.itemsize for x in operands + shapes)
    vmem = pl.BlockSpec(memory_space=pltpu.VMEM)
    result = pl.pallas_call(
        functools.partial(
            kernel_with_edges if edges is not None else kernel_without_edges,
            plan,
            field_at,
            partial is not None,
            target_off,
            emit,
            copies,
            tiles,
            extra,
        ),
        out_shape=tuple(shapes) if several else shapes[0],
        in_specs=[vmem] * len(operands),
        out_specs=tuple([vmem] * len(shapes)) if several else vmem,
        cost_estimate=pl.CostEstimate(flops=flops, bytes_accessed=moved, transcendentals=0),
    )(*operands)
    return result


def split_high_low(field):
    rounded = lax.reduce_precision(field, exponent_bits=8, mantissa_bits=7)
    return rounded.astype(jnp.bfloat16), (field - rounded).astype(jnp.bfloat16)


def own_plan(lat_blocks, members, fields, offsets):
    return tuple(
        tuple(
            (dr, members, p + dr - 1, fields[p + dr - 1], p + dr - 1 if len(set(fields)) == 1 else 0)
            + offsets
            + (0,)
            for dr in range(3)
            if 0 <= p + dr - 1 < lat_blocks
        )
        for p in range(lat_blocks)
    )


def halo_plan(lat_blocks, members, field, offsets, trimmed=False):
    return tuple(
        tuple(
            (dr, members[p + dr > 0], 0, field[p + dr > 0], 0)
            + offsets
            + ((1 if p + dr == 0 else 2) if trimmed else 0,)
            for dr in range(3)
            if not 0 <= p + dr - 1 < lat_blocks
        )
        for p in range(lat_blocks)
    )


def local(anomalies, panel, pair_code, pair_offset):
    del pair_code, pair_offset
    lat_blocks, lon_blocks = anomalies.shape[:2]
    taper = taper_by_code()
    panel_high, panel_low = split_high_low(panel)
    wider, west, east = lon_halo(jnp.concatenate([anomalies, panel_high, panel_low], axis=2), 2)
    kept = COLS - STRIDE
    going_north = jnp.concatenate(
        [wider[:1, :, :K], wider[:1, :, K : K + kept], wider[:1, :, K + COLS : K + COLS + kept]], axis=2
    )
    going_south = jnp.concatenate(
        [wider[-1:, :, :K], wider[-1:, :, K + STRIDE : K + COLS], wider[-1:, :, K + COLS + STRIDE :]], axis=2
    )
    north, south = lat_halo(going_north, going_south)
    targets = jnp.swapaxes(anomalies, 2, 3)
    edges = jnp.swapaxes(jnp.concatenate([west[:, 1:, :K, :], east[:, :1, :K, :]], axis=1), 2, 3)
    like_wide = jax.ShapeDtypeStruct((lat_blocks, lon_blocks + 2) + panel.shape[2:], jnp.float32)
    own_fields = (0,) * lat_blocks
    span = (1, lon_blocks + 3)
    partial, members, own_tiles = rows_call(
        own_plan(lat_blocks, 0, own_fields, (0, 0)),
        K,
        targets,
        taper,
        None,
        (wider,),
        like_wide,
        target_off=-1,
        edges=edges,
        copies=((0,) + span,),
        tiles="save",
    )
    emit = tuple(0 if p == 0 else 1 for p in range(lat_blocks))
    first_product, first_row, last_row, sent_north, sent_south = rows_call(
        halo_plan(lat_blocks, (0, 1), (0, 1), (0, 0), trimmed=True),
        K,
        targets,
        taper,
        partial,
        (north, south),
        panel,
        target_off=-1,
        emit=emit,
        edges=edges,
    )
    north2, south2 = lat_halo(sent_north, sent_south)
    row_fields = (1, 2) if lat_blocks == 2 else None
    partial, halo_tiles = rows_call(
        own_plan(lat_blocks, 0, row_fields, (0, 0)),
        0,
        targets,
        taper,
        None,
        (members, first_row, last_row, north, south, own_tiles),
        panel,
        tiles="load",
        extra=halo_plan(lat_blocks, (3, 4), (3, 4), (1, 0)),
    )
    second_product = rows_call(
        halo_plan(lat_blocks, (0, 1), (0, 1), (0, 0), trimmed=True),
        0,
        targets,
        taper,
        partial,
        (north2, south2, halo_tiles),
        panel,
        tiles="load",
    )
    return (first_product, second_product)


def solution(mesh):
    placed = (
        P("lat", "lon", None, None),
        P("lat", "lon", None, None),
        P("lat", "lon", None),
        P(None, "lat", "lon", None),
    )
    return jax.shard_map(
        local,
        mesh=mesh,
        in_specs=placed,
        out_specs=(P("lat", "lon", None, None), P("lat", "lon", None, None)),
        check_vma=False,
    )
```
